256 devices in a mesh: gx: 32 (over y, z_hi, core), gz: 8 (over z_lo, x).
Axes of the slice: x: 4, y: 4, z: 8 (z_hi: 4, z_lo: 2; z = z_hi * 2 + z_lo), core: 2. Of those that a mesh axis runs over, the one named last changes fastest.
Arguments:
- scalars: float32 [2, 4096, 128, 256], P(None, 'gx', 'gz'), may hold values from -6 to 6
- diffusivity: float32 [4096, 128, 256], P('gx', 'gz'), may hold values from 0.01 to 0.1
- reaction_rate: float32 [4096, 128, 256], P('gx', 'gz'), may hold values from 0.05 to 1
- block_inverse: float32 [2, 32, 128, 128], P(None, 'gx'), may hold values from 0 to 1
- block_response: float32 [2, 32, 128], P(None, 'gx'), may hold values from 0 to 1, as said below
- mean_profile: float32 [2, 256], replicated, may hold values from -4 to 4
- recycle_gain: float32 [2, 256], replicated, may hold values from 0.5 to 1.5
- station_index: int32 [1], replicated, may hold values from 0 to 4095
- span_shift: int32 [1], replicated, may hold values from 0 to 127
Outputs:
- transported: float32 [2, 4096, 128, 256], P(None, 'gx', 'gz')
The draws below stay inside these ranges and needn't reach their ends.
Inputs may be any that keep to these rules, and one draw needn't show every extreme that they name: `block_response`: every entry is positive.
All inputs are finite; a program needn't handle non-finite values.
Results may differ from the reference program's by a relative error of at most 0.0003.
Values sent between devices are 32-bit elements; how exact they have to be, the bound alone decides.
No kernel may reach another device: no remote copies, remote signals or barrier semaphores. Data moves between devices by JAX's collectives and lax.ppermute only.
A program may use at most 64 MiB of HBM per device.

```python
import math
import jax
import jax.numpy as jnp
from jax import lax

SPECIES_NUMBER = 2
SEGMENT_SLICES = 128
NY = 256
AXIAL_SLICES = 4096
NZ = 128


def decay_tables(key):
    child_seeds = jax.random.split(jax.random.fold_in(key, 11), 7)
    segment_slice_sum = AXIAL_SLICES // SEGMENT_SLICES
    shuffled = jax.random.permutation(child_seeds[0], SPECIES_NUMBER)
    slow_scalars = shuffled < (SPECIES_NUMBER + 1) // 2
    weight_low = 0.6
    device_factor = jnp.exp(jax.random.uniform(child_seeds[1], (SPECIES_NUMBER, segment_slice_sum, 1), minval=math.log(0.5), maxval=math.log(2.0)))
    plane_factor = jnp.exp(jax.random.uniform(child_seeds[2], (SPECIES_NUMBER, segment_slice_sum, SEGMENT_SLICES), minval=math.log(0.7), maxval=math.log(1.4)))
    slow_rate = 0.5 / AXIAL_SLICES * device_factor * plane_factor
    fast_rate = jnp.exp(jax.random.uniform(child_seeds[3], (SPECIES_NUMBER, segment_slice_sum, SEGMENT_SLICES), minval=math.log(2.5 / SEGMENT_SLICES), maxval=math.log(4.3 / SEGMENT_SLICES))) * jnp.sqrt(device_factor)
    attenuation_speed = jnp.where(slow_scalars[:, None, None], slow_rate, fast_rate)
    slice_positions = jax.random.randint(child_seeds[4], (SPECIES_NUMBER, 2), 0, AXIAL_SLICES)
    slice_entries = jnp.arange(AXIAL_SLICES, dtype=jnp.int32)
    pulse_onset_times = jnp.sum((slice_entries[None, None, :] == slice_positions[:, :, None]).astype(jnp.float32), axis=1)
    pulse_strength = jax.random.uniform(child_seeds[5], (SPECIES_NUMBER, AXIAL_SLICES), minval=0.2, maxval=0.4)
    attenuation_speed = attenuation_speed + (pulse_onset_times * -jnp.log1p(-pulse_strength)).reshape(SPECIES_NUMBER, segment_slice_sum, SEGMENT_SLICES)
    source_weight = jax.random.uniform(child_seeds[6], (SPECIES_NUMBER, segment_slice_sum, SEGMENT_SLICES), minval=weight_low, maxval=1.0)
    cumulative = jnp.cumsum(attenuation_speed, axis=-1)
    separation = cumulative[..., :, None] - cumulative[..., None, :]
    lower = slice_entries[:SEGMENT_SLICES, None] >= slice_entries[None, :SEGMENT_SLICES]
    gain_part = -jnp.expm1(-attenuation_speed) * source_weight
    inverse_table = jnp.where(lower, jnp.exp(-jnp.maximum(separation, 0.0)) * gain_part[..., None, :], 0.0)
    response_table = jnp.exp(-cumulative)
    return (inverse_table.astype(jnp.float32), response_table.astype(jnp.float32))


def draw_block_inverse(key, part):
    return decay_tables(key)[0]


def draw_block_response(key, part):
    return decay_tables(key)[1]


def level_of(stream_key, shape, pieces, smallest, top_value):
    def one(dim, shards_of):
        steps = jax.random.uniform(jax.random.fold_in(jax.random.fold_in(stream_key, 6), dim), (shards_of,), jnp.float32, smallest / len(pieces), top_value / len(pieces))
        return jnp.repeat(jnp.exp(steps), shape[dim] // shards_of).reshape((-1,) + (1,) * (len(shape) - dim - 1))

    gain = one(*pieces[0])
    for cut in pieces[1:]:
        gain = gain * one(*cut)
    return gain


def gaussian(rng, shape, spread, bound, pieces=(), kind=jnp.bfloat16):
    values = spread * jax.random.normal(rng, shape, jnp.float32)
    if pieces:
        values = values * level_of(rng, shape, pieces, -0.22, 0.18)
    return jnp.clip(values, -bound, bound).astype(kind)


def setup_inputs(seed: int = 0) -> dict:
    splits = jax.random.split(jax.random.key(seed), 10)
    scalars = gaussian(splits[0], (SPECIES_NUMBER, AXIAL_SLICES, NZ, NY), 1.0, 6.0, ((1, 32), (2, 8)), jnp.float32)
    diffusivity = jnp.clip(jnp.exp(math.log(0.1) - 2.3025851 * jax.random.uniform(splits[1], (AXIAL_SLICES, NZ, NY), jnp.float32) ** level_of(splits[1], (AXIAL_SLICES, NZ, NY), ((0, 32), (1, 8)), -0.2, 0.2)), 0.01, 0.1)
    reaction_rate = jnp.clip(jnp.exp(math.log(1.0) - 2.9957323 * jax.random.uniform(splits[2], (AXIAL_SLICES, NZ, NY), jnp.float32) ** level_of(splits[2], (AXIAL_SLICES, NZ, NY), ((0, 32), (1, 8)), -0.2, 0.2)), 0.05, 1.0)
    block_inverse = draw_block_inverse(jax.random.fold_in(splits[9], 71), 0)
    block_response = draw_block_response(jax.random.fold_in(splits[9], 71), 0)
    mean_profile = gaussian(splits[5], (SPECIES_NUMBER, NY), 1.0, 4.0, (), jnp.float32)
    recycle_gain = jnp.clip(1.0 + 0.1 * jax.random.normal(splits[6], (SPECIES_NUMBER, NY), jnp.float32), 0.5, 1.5)
    station_index = jax.random.randint(splits[7], (1,), 0, AXIAL_SLICES).astype(jnp.int32)
    span_shift = jax.random.randint(splits[8], (1,), 0, NZ).astype(jnp.int32)
    return dict(scalars=scalars, diffusivity=diffusivity, reaction_rate=reaction_rate, block_inverse=block_inverse, block_response=block_response, mean_profile=mean_profile, recycle_gain=recycle_gain, station_index=station_index, span_shift=span_shift)


reaction_yields = (-1.0, 1.0)


def fourth_order(padded, dimension, length):
    def shifted(offset):
        return lax.slice_in_dim(padded, offset, offset + length, axis=dimension)
    return (-shifted(0) + 16.0 * shifted(1) - 30.0 * shifted(2) + 16.0 * shifted(3) - shifted(4)) / 12.0


def make_inflow(station_plane, mean_profile, recycle_gain, span_shift):
    span_mean = jnp.mean(station_plane, axis=1, keepdims=True)
    rolled = jnp.roll(station_plane, span_shift[0], axis=1)
    return mean_profile[:, None, :] + recycle_gain[:, None, :] * (rolled - span_mean)


def explicit_part(stream_padded, span_padded, center, diffusivity, reaction_rate):
    wall_padded = jnp.pad(center, ((0, 0), (0, 0), (0, 0), (2, 2)))
    laplacian = fourth_order(stream_padded, 1, center.shape[1])
    laplacian = laplacian + fourth_order(span_padded, 2, center.shape[2])
    laplacian = laplacian + fourth_order(wall_padded, 3, center.shape[3])
    reaction = reaction_rate * jax.nn.softplus(center[0]) * jax.nn.softplus(center[1])
    source = jnp.stack([reaction_yields[0] * reaction, reaction_yields[1] * reaction])
    return center + diffusivity[None] * laplacian + source


def reference(scalars, diffusivity, reaction_rate, block_inverse, block_response, mean_profile, recycle_gain, station_index, span_shift):
    station_plane = lax.dynamic_index_in_dim(scalars, station_index[0].astype(jnp.int32), axis=1, keepdims=False)
    inflow = make_inflow(station_plane, mean_profile, recycle_gain, span_shift)
    segment_slice_sum = block_inverse.shape[1]
    plane_count = block_inverse.shape[2]
    inlet_planes = jnp.broadcast_to(inflow[:, None], (SPECIES_NUMBER, 2, NZ, NY))
    outlet_planes = jnp.broadcast_to(scalars[:, -1:], (SPECIES_NUMBER, 2, NZ, NY))
    extended = jnp.concatenate([inlet_planes, scalars, outlet_planes], axis=1)

    def advance(running, block_id):
        first_row = (block_id * plane_count).astype(jnp.int32)
        window = lax.dynamic_slice_in_dim(extended, first_row, plane_count + 4, 1)
        center = lax.slice_in_dim(window, 2, 2 + plane_count, axis=1)
        span_padded = jnp.pad(center, ((0, 0), (0, 0), (2, 2), (0, 0)), mode="wrap")
        diff_block = lax.dynamic_slice_in_dim(diffusivity, first_row, plane_count, 0)
        rate_block = lax.dynamic_slice_in_dim(reaction_rate, first_row, plane_count, 0)
        explicit = explicit_part(window, span_padded, center, diff_block, rate_block)
        inverse = lax.dynamic_index_in_dim(block_inverse, block_id, 1, keepdims=False)
        response = lax.dynamic_index_in_dim(block_response, block_id, 1, keepdims=False)
        local_part = jnp.einsum("sij,sjzy->sizy", inverse, explicit, precision=lax.Precision.HIGHEST)
        result = local_part + response[:, :, None, None] * running[:, None]
        return result[:, -1], result

    last_plane, blocks = lax.scan(advance, inflow, jnp.arange(segment_slice_sum, dtype=jnp.int32))
    return jnp.moveaxis(blocks, 0, 1).reshape(SPECIES_NUMBER, AXIAL_SLICES, NZ, NY)
```

```python
import jax
import jax.numpy as jnp
from jax import lax
from jax.sharding import PartitionSpec as P

reaction_yields = (-1.0, 1.0)


def xor_sum(x, axis):
    devices = lax.axis_size(axis)
    step = 1
    while step < devices:
        pairs = [(i, i ^ step) for i in range(devices)]
        x = x + lax.ppermute(x, axis, pairs)
        step *= 2
    return x


def xor_gather(x, axis, dim):
    devices = lax.axis_size(axis)
    place = lax.axis_index(axis)
    step = 1
    while step < devices:
        pairs = [(i, i ^ step) for i in range(devices)]
        other = lax.ppermute(x, axis, pairs)
        low = (place & step) == 0
        x = jnp.where(
            low, jnp.concatenate([x, other], dim), jnp.concatenate([other, x], dim)
        )
        step *= 2
    return x


def compose(earlier, later):
    return (earlier[0] * later[0], later[0][:, None, None] * earlier[1] + later[1])


def exclusive_scan(part, axis):
    devices = lax.axis_size(axis)
    place = lax.axis_index(axis)
    total = part
    before = (jnp.ones_like(part[0]), jnp.zeros_like(part[1]))
    step = 1
    while step < devices:
        pairs = [(i, i ^ step) for i in range(devices)]
        other = lax.ppermute(total, axis, pairs)
        later = (place & step) != 0
        new_before = compose(other, before)
        before = jax.tree.map(lambda a, b: jnp.where(later, a, b), new_before, before)
        total = jax.tree.map(
            lambda a, b: jnp.where(later, a, b), compose(other, total), compose(total, other)
        )
        step *= 2
    return before


def with_halo(x, sides, width, wrap):
    for axis, dim in sides:
        devices, length = (lax.axis_size(axis), x.shape[dim])
        up = [(i, (i + 1) % devices) for i in range(devices if wrap else devices - 1)]
        down = [(j, i) for i, j in up]
        last = lax.slice_in_dim(x, length - width, length, axis=dim)
        first = lax.slice_in_dim(x, 0, width, axis=dim)
        before = lax.ppermute(last, axis, up)
        after = lax.ppermute(first, axis, down)
        x = jnp.concatenate([before, x, after], axis=dim)
    return x


def fourth_order(padded, dimension, length):

    def shifted(offset):
        return lax.slice_in_dim(padded, offset, offset + length, axis=dimension)

    return (
        -shifted(0) + 16.0 * shifted(1) - 30.0 * shifted(2) + 16.0 * shifted(3) - shifted(4)
    ) / 12.0


def make_inflow(station_plane, mean_profile, recycle_gain, span_shift):
    span_mean = jnp.mean(station_plane, axis=1, keepdims=True)
    rolled = jnp.roll(station_plane, span_shift[0], axis=1)
    return mean_profile[:, None, :] + recycle_gain[:, None, :] * (rolled - span_mean)


def explicit_part(stream_padded, span_padded, center, diffusivity, reaction_rate):
    wall_padded = jnp.pad(center, ((0, 0), (0, 0), (0, 0), (2, 2)))
    laplacian = fourth_order(stream_padded, 1, center.shape[1])
    laplacian = laplacian + fourth_order(span_padded, 2, center.shape[2])
    laplacian = laplacian + fourth_order(wall_padded, 3, center.shape[3])
    reaction = reaction_rate * jax.nn.softplus(center[0]) * jax.nn.softplus(center[1])
    source = jnp.stack([reaction_yields[0] * reaction, reaction_yields[1] * reaction])
    return center + diffusivity[None] * laplacian + source


def on_device(
    scalars,
    diffusivity,
    reaction_rate,
    block_inverse,
    block_response,
    mean_profile,
    recycle_gain,
    station_index,
    span_shift,
):
    plane_count = scalars.shape[1]
    span_cells = scalars.shape[2]
    stream_devices = lax.axis_size("gx")
    stream_rank = lax.axis_index("gx")
    span_rank = lax.axis_index("gz")
    owner_row = station_index[0] // plane_count
    local_plane = station_index[0] - owner_row * plane_count
    own_slice = lax.dynamic_index_in_dim(scalars, local_plane, 1, keepdims=False)
    mine = stream_rank == owner_row
    arrived = xor_sum(jnp.where(mine, own_slice, jnp.zeros_like(own_slice)), "gx")
    station_plane = xor_gather(arrived, "gz", 1)
    inflow_full = make_inflow(station_plane, mean_profile, recycle_gain, span_shift)
    inflow = lax.dynamic_slice_in_dim(inflow_full, span_rank * span_cells, span_cells, 1)
    stream_padded = with_halo(scalars, (("gx", 1),), 2, False)
    edge_shape = (scalars.shape[0], 2, scalars.shape[2], scalars.shape[3])
    inlet_planes = jnp.broadcast_to(inflow[:, None], edge_shape)
    outlet_planes = jnp.broadcast_to(scalars[:, -1:], edge_shape)
    head_planes = jnp.where(stream_rank == 0, inlet_planes, stream_padded[:, :2])
    tail_planes = jnp.where(stream_rank == stream_devices - 1, outlet_planes, stream_padded[:, -2:])
    window = jnp.concatenate([head_planes, stream_padded[:, 2:-2], tail_planes], axis=1)
    span_padded = with_halo(scalars, (("gz", 2),), 2, True)
    explicit = explicit_part(window, span_padded, scalars, diffusivity, reaction_rate)
    inverse = block_inverse[:, 0]
    response = block_response[:, 0]
    exit_plane = jnp.einsum(
        "sj,sjzy->szy", inverse[:, -1], explicit, precision=lax.Precision.HIGHEST
    )
    exit_ratio = response[:, -1]
    through, upstream_sum = exclusive_scan((exit_ratio, exit_plane), "gx")
    incoming = through[:, None, None] * inflow + upstream_sum
    local_part = jnp.einsum(
        "sij,sjzy->sizy", inverse, explicit, precision=lax.Precision.HIGHEST
    )
    return local_part + response[:, :, None, None] * incoming[:, None]


def solution(mesh):
    return jax.shard_map(
        on_device,
        mesh=mesh,
        in_specs=(
            P(None, "gx", "gz", None),
            P("gx", "gz", None),
            P("gx", "gz", None),
            P(None, "gx", None, None),
            P(None, "gx", None),
            P(),
            P(),
            P(),
            P(),
        ),
        out_specs=P(None, "gx", "gz", None),
        check_vma=False,
    )
```

```python
import jax
import jax.numpy as jnp
from jax import lax
from jax.sharding import PartitionSpec as P

reaction_yields = (-1.0, 1.0)


def xor_sum(x, axis):
    devices = lax.axis_size(axis)
    step = 1
    while step < devices:
        pairs = [(i, i ^ step) for i in range(devices)]
        x = x + lax.ppermute(x, axis, pairs)
        step *= 2
    return x


def xor_gather(x, axis, dim):
    devices = lax.axis_size(axis)
    place = lax.axis_index(axis)
    step = 1
    while step < devices:
        pairs = [(i, i ^ step) for i in range(devices)]
        other = lax.ppermute(x, axis, pairs)
        low = (place & step) == 0
        x = jnp.where(
            low, jnp.concatenate([x, other], dim), jnp.concatenate([other, x], dim)
        )
        step *= 2
    return x


def compose(earlier, later):
    return (later[0] * earlier[0], later[0] * earlier[1] + later[1])


def exclusive_scan(part, axis):
    devices = lax.axis_size(axis)
    place = lax.axis_index(axis)
    total = part
    before = (jnp.ones_like(part[0]), jnp.zeros_like(part[1]))
    step = 1
    while step < devices:
        pairs = [(i, i ^ step) for i in range(devices)]
        other = lax.ppermute(jnp.stack(total), axis, pairs)
        other = (other[0], other[1])
        later = (place & step) != 0
        new_before = compose(other, before)
        before = jax.tree.map(lambda a, b: jnp.where(later, a, b), new_before, before)
        total = jax.tree.map(
            lambda a, b: jnp.where(later, a, b), compose(other, total), compose(total, other)
        )
        step *= 2
    return before


def with_halo(x, sides, width, wrap):
    for axis, dim in sides:
        devices, length = (lax.axis_size(axis), x.shape[dim])
        up = [(i, (i + 1) % devices) for i in range(devices if wrap else devices - 1)]
        down = [(j, i) for i, j in up]
        last = lax.slice_in_dim(x, length - width, length, axis=dim)
        first = lax.slice_in_dim(x, 0, width, axis=dim)
        before = lax.ppermute(last, axis, up)
        after = lax.ppermute(first, axis, down)
        x = jnp.concatenate([before, x, after], axis=dim)
    return x


def fourth_order(padded, dimension, length):

    def shifted(offset):
        return lax.slice_in_dim(padded, offset, offset + length, axis=dimension)

    return (
        -shifted(0) + 16.0 * shifted(1) - 30.0 * shifted(2) + 16.0 * shifted(3) - shifted(4)
    ) / 12.0


def make_inflow(station_plane, mean_profile, recycle_gain, span_shift):
    span_mean = jnp.mean(station_plane, axis=1, keepdims=True)
    rolled = jnp.roll(station_plane, span_shift[0], axis=1)
    return mean_profile[:, None, :] + recycle_gain[:, None, :] * (rolled - span_mean)


def explicit_part(stream_padded, span_padded, center, diffusivity, reaction_rate):
    wall_padded = jnp.pad(center, ((0, 0), (0, 0), (0, 0), (2, 2)))
    laplacian = fourth_order(stream_padded, 1, center.shape[1])
    laplacian = laplacian + fourth_order(span_padded, 2, center.shape[2])
    laplacian = laplacian + fourth_order(wall_padded, 3, center.shape[3])
    reaction = reaction_rate * jax.nn.softplus(center[0]) * jax.nn.softplus(center[1])
    source = jnp.stack([reaction_yields[0] * reaction, reaction_yields[1] * reaction])
    return center + diffusivity[None] * laplacian + source


def on_device(
    scalars,
    diffusivity,
    reaction_rate,
    block_inverse,
    block_response,
    mean_profile,
    recycle_gain,
    station_index,
    span_shift,
):
    plane_count = scalars.shape[1]
    span_cells = scalars.shape[2]
    stream_devices = lax.axis_size("gx")
    stream_rank = lax.axis_index("gx")
    span_rank = lax.axis_index("gz")
    at_inlet = stream_rank == 0
    owner_row = station_index[0] // plane_count
    local_plane = station_index[0] - owner_row * plane_count
    own_slice = lax.dynamic_index_in_dim(scalars, local_plane, 1, keepdims=False)
    mine = stream_rank == owner_row
    arrived = xor_sum(jnp.where(mine, own_slice, jnp.zeros_like(own_slice)), "gx")
    station_plane = xor_gather(arrived, "gz", 1)
    inflow_full = make_inflow(station_plane, mean_profile, recycle_gain, span_shift)
    inflow = lax.dynamic_slice_in_dim(inflow_full, span_rank * span_cells, span_cells, 1)
    stream_padded = with_halo(scalars, (("gx", 1),), 2, False)
    edge_shape = (scalars.shape[0], 2, scalars.shape[2], scalars.shape[3])
    outlet_planes = jnp.broadcast_to(scalars[:, -1:], edge_shape)
    head_planes = jnp.where(at_inlet, jnp.zeros(edge_shape, scalars.dtype), stream_padded[:, :2])
    tail_planes = jnp.where(stream_rank == stream_devices - 1, outlet_planes, stream_padded[:, -2:])
    window = jnp.concatenate([head_planes, stream_padded[:, 2:-2], tail_planes], axis=1)
    span_padded = with_halo(scalars, (("gz", 2),), 2, True)
    explicit = explicit_part(window, span_padded, scalars, diffusivity, reaction_rate)
    inverse = block_inverse[:, 0]
    response = block_response[:, 0]
    first_gain = jnp.where(at_inlet, diffusivity[0] * (15.0 / 12.0), 0.0)
    second_gain = jnp.where(at_inlet, diffusivity[1] * (-1.0 / 12.0), 0.0)
    exit_plane = jnp.einsum(
        "sj,sjzy->szy", inverse[:, -1], explicit, precision=lax.Precision.HIGHEST
    )
    exit_gain = (
        response[:, -1][:, None, None]
        + inverse[:, -1, 0][:, None, None] * first_gain
        + inverse[:, -1, 1][:, None, None] * second_gain
    )
    through, upstream_sum = exclusive_scan((exit_gain, exit_plane), "gx")
    incoming = through * inflow + upstream_sum
    local_part = jnp.einsum(
        "sij,sjzy->sizy", inverse, explicit, precision=lax.Precision.HIGHEST
    )
    first_in = first_gain * inflow
    second_in = second_gain * inflow
    return (
        local_part
        + response[:, :, None, None] * incoming[:, None]
        + inverse[:, :, 0][:, :, None, None] * first_in[:, None]
        + inverse[:, :, 1][:, :, None, None] * second_in[:, None]
    )


def solution(mesh):
    return jax.shard_map(
        on_device,
        mesh=mesh,
        in_specs=(
            P(None, "gx", "gz", None),
            P("gx", "gz", None),
            P("gx", "gz", None),
            P(None, "gx", None, None),
            P(None, "gx", None),
            P(),
            P(),
            P(),
            P(),
        ),
        out_specs=P(None, "gx", "gz", None),
        check_vma=False,
    )
```

```python
import jax
import jax.numpy as jnp
from jax import lax
from jax.sharding import PartitionSpec as P

reaction_yields = (-1.0, 1.0)


def xor_sum(x, axis):
    devices = lax.axis_size(axis)
    step = 1
    while step < devices:
        pairs = [(i, i ^ step) for i in range(devices)]
        x = x + lax.ppermute(x, axis, pairs)
        step *= 2
    return x


def xor_gather(x, axis, dim):
    devices = lax.axis_size(axis)
    place = lax.axis_index(axis)
    step = 1
    while step < devices:
        pairs = [(i, i ^ step) for i in range(devices)]
        other = lax.ppermute(x, axis, pairs)
        low = (place & step) == 0
        x = jnp.where(
            low, jnp.concatenate([x, other], dim), jnp.concatenate([other, x], dim)
        )
        step *= 2
    return x


def compose(earlier, later):
    return (later[0] * earlier[0], later[0] * earlier[1] + later[1])


def exclusive_scan(part, axis):
    devices = lax.axis_size(axis)
    place = lax.axis_index(axis)
    total = part
    before = (jnp.ones_like(part[0]), jnp.zeros_like(part[1]))
    step = 1
    while step < devices:
        pairs = [(i, i ^ step) for i in range(devices)]
        other = lax.ppermute(jnp.stack(total), axis, pairs)
        other = (other[0], other[1])
        later = (place & step) != 0
        new_before = compose(other, before)
        before = jax.tree.map(lambda a, b: jnp.where(later, a, b), new_before, before)
        total = jax.tree.map(
            lambda a, b: jnp.where(later, a, b), compose(other, total), compose(total, other)
        )
        step *= 2
    return before


def with_halo(x, sides, width, wrap):
    for axis, dim in sides:
        devices, length = (lax.axis_size(axis), x.shape[dim])
        up = [(i, (i + 1) % devices) for i in range(devices if wrap else devices - 1)]
        down = [(j, i) for i, j in up]
        last = lax.slice_in_dim(x, length - width, length, axis=dim)
        first = lax.slice_in_dim(x, 0, width, axis=dim)
        before = lax.ppermute(last, axis, up)
        after = lax.ppermute(first, axis, down)
        x = jnp.concatenate([before, x, after], axis=dim)
    return x


def fourth_order(padded, dimension, length):

    def shifted(offset):
        return lax.slice_in_dim(padded, offset, offset + length, axis=dimension)

    return (
        -shifted(0) + 16.0 * shifted(1) - 30.0 * shifted(2) + 16.0 * shifted(3) - shifted(4)
    ) / 12.0


def make_inflow(station_plane, mean_profile, recycle_gain, span_shift):
    span_mean = jnp.mean(station_plane, axis=1, keepdims=True)
    rolled = jnp.roll(station_plane, span_shift[0], axis=1)
    return mean_profile[:, None, :] + recycle_gain[:, None, :] * (rolled - span_mean)


def explicit_part(stream_padded, span_padded, center, diffusivity, reaction_rate):
    wall_padded = jnp.pad(center, ((0, 0), (0, 0), (0, 0), (2, 2)))
    laplacian = fourth_order(stream_padded, 1, center.shape[1])
    laplacian = laplacian + fourth_order(span_padded, 2, center.shape[2])
    laplacian = laplacian + fourth_order(wall_padded, 3, center.shape[3])
    reaction = reaction_rate * jax.nn.softplus(center[0]) * jax.nn.softplus(center[1])
    source = jnp.stack([reaction_yields[0] * reaction, reaction_yields[1] * reaction])
    return center + diffusivity[None] * laplacian + source


def on_device(
    scalars,
    diffusivity,
    reaction_rate,
    block_inverse,
    block_response,
    mean_profile,
    recycle_gain,
    station_index,
    span_shift,
):
    plane_count = scalars.shape[1]
    span_cells = scalars.shape[2]
    stream_devices = lax.axis_size("gx")
    stream_rank = lax.axis_index("gx")
    span_rank = lax.axis_index("gz")
    at_inlet = stream_rank == 0
    owner_row = station_index[0] // plane_count
    local_plane = station_index[0] - owner_row * plane_count
    own_slice = lax.dynamic_index_in_dim(scalars, local_plane, 1, keepdims=False)
    mine = stream_rank == owner_row
    candidate = jnp.where(mine, own_slice, jnp.zeros_like(own_slice))
    stream_padded = with_halo(scalars, (("gx", 1),), 2, False)
    edge_shape = (scalars.shape[0], 2, scalars.shape[2], scalars.shape[3])
    outlet_planes = jnp.broadcast_to(scalars[:, -1:], edge_shape)
    head_planes = jnp.where(at_inlet, jnp.zeros(edge_shape, scalars.dtype), stream_padded[:, :2])
    tail_planes = jnp.where(stream_rank == stream_devices - 1, outlet_planes, stream_padded[:, -2:])
    window = jnp.concatenate([head_planes, stream_padded[:, 2:-2], tail_planes], axis=1)
    span_padded = with_halo(scalars, (("gz", 2),), 2, True)
    explicit = explicit_part(window, span_padded, scalars, diffusivity, reaction_rate)
    candidate, explicit = lax.optimization_barrier((candidate, explicit))
    arrived = xor_sum(candidate, "gx")
    station_plane = xor_gather(arrived, "gz", 1)
    inflow_full = make_inflow(station_plane, mean_profile, recycle_gain, span_shift)
    inflow = lax.dynamic_slice_in_dim(inflow_full, span_rank * span_cells, span_cells, 1)
    inverse = block_inverse[:, 0]
    response = block_response[:, 0]
    first_gain = jnp.where(at_inlet, diffusivity[0] * (15.0 / 12.0), 0.0)
    second_gain = jnp.where(at_inlet, diffusivity[1] * (-1.0 / 12.0), 0.0)
    exit_plane = jnp.einsum(
        "sj,sjzy->szy", inverse[:, -1], explicit, precision=lax.Precision.HIGHEST
    )
    exit_gain = (
        response[:, -1][:, None, None]
        + inverse[:, -1, 0][:, None, None] * first_gain
        + inverse[:, -1, 1][:, None, None] * second_gain
    )
    through, upstream_sum = exclusive_scan((exit_gain, exit_plane), "gx")
    incoming = through * inflow + upstream_sum
    local_part = jnp.einsum(
        "sij,sjzy->sizy", inverse, explicit, precision=lax.Precision.HIGHEST
    )
    first_in = first_gain * inflow
    second_in = second_gain * inflow
    return (
        local_part
        + response[:, :, None, None] * incoming[:, None]
        + inverse[:, :, 0][:, :, None, None] * first_in[:, None]
        + inverse[:, :, 1][:, :, None, None] * second_in[:, None]
    )


def solution(mesh):
    return jax.shard_map(
        on_device,
        mesh=mesh,
        in_specs=(
            P(None, "gx", "gz", None),
            P("gx", "gz", None),
            P("gx", "gz", None),
            P(None, "gx", None, None),
            P(None, "gx", None),
            P(),
            P(),
            P(),
            P(),
        ),
        out_specs=P(None, "gx", "gz", None),
        check_vma=False,
    )
```

```python
import jax
import jax.numpy as jnp
from jax import lax
from jax.sharding import PartitionSpec as P

reaction_yields = (-1.0, 1.0)


def xor_sum(x, axis):
    devices = lax.axis_size(axis)
    step = 1
    while step < devices:
        pairs = [(i, i ^ step) for i in range(devices)]
        x = x + lax.ppermute(x, axis, pairs)
        step *= 2
    return x


def xor_gather(x, axis, dim):
    devices = lax.axis_size(axis)
    place = lax.axis_index(axis)
    step = 1
    while step < devices:
        pairs = [(i, i ^ step) for i in range(devices)]
        other = lax.ppermute(x, axis, pairs)
        low = (place & step) == 0
        x = jnp.where(
            low, jnp.concatenate([x, other], dim), jnp.concatenate([other, x], dim)
        )
        step *= 2
    return x


def compose(earlier, later):
    return (later[0] * earlier[0], later[0] * earlier[1] + later[1])


def exclusive_scan(part, carried, axis):
    devices = lax.axis_size(axis)
    place = lax.axis_index(axis)
    total = part
    before = (jnp.ones_like(part[0]), jnp.zeros_like(part[1]))
    step = 1
    while step < devices:
        pairs = [(i, i ^ step) for i in range(devices)]
        other = lax.ppermute(jnp.stack(total + (carried,)), axis, pairs)
        carried = carried + other[2]
        other = (other[0], other[1])
        later = (place & step) != 0
        new_before = compose(other, before)
        before = jax.tree.map(lambda a, b: jnp.where(later, a, b), new_before, before)
        total = jax.tree.map(
            lambda a, b: jnp.where(later, a, b), compose(other, total), compose(total, other)
        )
        step *= 2
    return before, carried


def with_halo(x, sides, width, wrap):
    for axis, dim in sides:
        devices, length = (lax.axis_size(axis), x.shape[dim])
        up = [(i, (i + 1) % devices) for i in range(devices if wrap else devices - 1)]
        down = [(j, i) for i, j in up]
        last = lax.slice_in_dim(x, length - width, length, axis=dim)
        first = lax.slice_in_dim(x, 0, width, axis=dim)
        before = lax.ppermute(last, axis, up)
        after = lax.ppermute(first, axis, down)
        x = jnp.concatenate([before, x, after], axis=dim)
    return x


def fourth_order(padded, dimension, length):

    def shifted(offset):
        return lax.slice_in_dim(padded, offset, offset + length, axis=dimension)

    return (
        -shifted(0) + 16.0 * shifted(1) - 30.0 * shifted(2) + 16.0 * shifted(3) - shifted(4)
    ) / 12.0


def make_inflow(station_plane, mean_profile, recycle_gain, span_shift):
    span_mean = jnp.mean(station_plane, axis=1, keepdims=True)
    rolled = jnp.roll(station_plane, span_shift[0], axis=1)
    return mean_profile[:, None, :] + recycle_gain[:, None, :] * (rolled - span_mean)


def explicit_part(stream_padded, span_padded, center, diffusivity, reaction_rate):
    wall_padded = jnp.pad(center, ((0, 0), (0, 0), (0, 0), (2, 2)))
    laplacian = fourth_order(stream_padded, 1, center.shape[1])
    laplacian = laplacian + fourth_order(span_padded, 2, center.shape[2])
    laplacian = laplacian + fourth_order(wall_padded, 3, center.shape[3])
    reaction = reaction_rate * jax.nn.softplus(center[0]) * jax.nn.softplus(center[1])
    source = jnp.stack([reaction_yields[0] * reaction, reaction_yields[1] * reaction])
    return center + diffusivity[None] * laplacian + source


def on_device(
    scalars,
    diffusivity,
    reaction_rate,
    block_inverse,
    block_response,
    mean_profile,
    recycle_gain,
    station_index,
    span_shift,
):
    plane_count = scalars.shape[1]
    span_cells = scalars.shape[2]
    stream_devices = lax.axis_size("gx")
    stream_rank = lax.axis_index("gx")
    span_rank = lax.axis_index("gz")
    at_inlet = stream_rank == 0
    owner_row = station_index[0] // plane_count
    local_plane = station_index[0] - owner_row * plane_count
    own_slice = lax.dynamic_index_in_dim(scalars, local_plane, 1, keepdims=False)
    mine = stream_rank == owner_row
    station_plane = xor_gather(own_slice, "gz", 1)
    inflow_full = make_inflow(station_plane, mean_profile, recycle_gain, span_shift)
    own_inflow = lax.dynamic_slice_in_dim(inflow_full, span_rank * span_cells, span_cells, 1)
    candidate = jnp.where(mine, own_inflow, jnp.zeros_like(own_inflow))
    stream_padded = with_halo(scalars, (("gx", 1),), 2, False)
    edge_shape = (scalars.shape[0], 2, scalars.shape[2], scalars.shape[3])
    outlet_planes = jnp.broadcast_to(scalars[:, -1:], edge_shape)
    head_planes = jnp.where(at_inlet, jnp.zeros(edge_shape, scalars.dtype), stream_padded[:, :2])
    tail_planes = jnp.where(stream_rank == stream_devices - 1, outlet_planes, stream_padded[:, -2:])
    window = jnp.concatenate([head_planes, stream_padded[:, 2:-2], tail_planes], axis=1)
    span_padded = with_halo(scalars, (("gz", 2),), 2, True)
    explicit = explicit_part(window, span_padded, scalars, diffusivity, reaction_rate)
    inverse = block_inverse[:, 0]
    response = block_response[:, 0]
    first_gain = jnp.where(at_inlet, diffusivity[0] * (15.0 / 12.0), 0.0)
    second_gain = jnp.where(at_inlet, diffusivity[1] * (-1.0 / 12.0), 0.0)
    exit_plane = jnp.einsum(
        "sj,sjzy->szy", inverse[:, -1], explicit, precision=lax.Precision.HIGHEST
    )
    exit_gain = (
        response[:, -1][:, None, None]
        + inverse[:, -1, 0][:, None, None] * first_gain
        + inverse[:, -1, 1][:, None, None] * second_gain
    )
    (through, upstream_sum), inflow = exclusive_scan((exit_gain, exit_plane), candidate, "gx")
    incoming = through * inflow + upstream_sum
    local_part = jnp.einsum(
        "sij,sjzy->sizy", inverse, explicit, precision=lax.Precision.HIGHEST
    )
    first_in = first_gain * inflow
    second_in = second_gain * inflow
    return (
        local_part
        + response[:, :, None, None] * incoming[:, None]
        + inverse[:, :, 0][:, :, None, None] * first_in[:, None]
        + inverse[:, :, 1][:, :, None, None] * second_in[:, None]
    )


def solution(mesh):
    return jax.shard_map(
        on_device,
        mesh=mesh,
        in_specs=(
            P(None, "gx", "gz", None),
            P("gx", "gz", None),
            P("gx", "gz", None),
            P(None, "gx", None, None),
            P(None, "gx", None),
            P(),
            P(),
            P(),
            P(),
        ),
        out_specs=P(None, "gx", "gz", None),
        check_vma=False,
    )
```

```python
import functools

import jax
import jax.numpy as jnp
from jax import lax
from jax.experimental import pallas as pl
from jax.experimental.pallas import tpu as pltpu
from jax.sharding import PartitionSpec as P

reaction_yields = (-1.0, 1.0)


def softplus(v):
    return jnp.maximum(v, 0.0) + jnp.log1p(jnp.exp(-jnp.abs(v)))


def explicit_kernel(planes, rows, width,
                    s_ref, head_ref, tail_ref, before_ref, after_ref, diff_ref, rate_ref, inv_ref,
                    out_ref, exit_ref, ex_ref):
    row = lax.broadcasted_iota(jnp.int32, (rows, width), 0)
    lane = lax.broadcasted_iota(jnp.int32, (rows, width), 1)

    def plane(s, k):
        if isinstance(k, int) and k < 0:
            return head_ref[s, pl.ds((k + 2) * rows, rows), :]
        if isinstance(k, int) and k >= planes:
            return tail_ref[s, pl.ds((k - planes) * rows, rows), :]
        start = k * rows if isinstance(k, int) else pl.multiple_of(k * rows, rows)
        return s_ref[s, pl.ds(start, rows), :]

    def halo_row(ref, s, j, r):
        return jnp.broadcast_to(ref[s, j, pl.ds(r, 1), :], (rows, width))

    def one_plane(j, jm2, jm1, jp1, jp2):
        centers = []
        laps = []
        for s in range(2):
            c = plane(s, j)
            sm2, sm1, sp1, sp2 = plane(s, jm2), plane(s, jm1), plane(s, jp1), plane(s, jp2)
            b0, b1 = halo_row(before_ref, s, j, 0), halo_row(before_ref, s, j, 1)
            a0, a1 = halo_row(after_ref, s, j, 0), halo_row(after_ref, s, j, 1)
            zm1 = jnp.where(row == 0, b1, pltpu.roll(c, 1, 0))
            zm2 = jnp.where(row == 0, b0, jnp.where(row == 1, b1, pltpu.roll(c, 2, 0)))
            zp1 = jnp.where(row == rows - 1, a0, pltpu.roll(c, rows - 1, 0))
            zp2 = jnp.where(row == rows - 1, a1, jnp.where(row == rows - 2, a0, pltpu.roll(c, rows - 2, 0)))
            ym1 = jnp.where(lane < 1, 0.0, pltpu.roll(c, 1, 1))
            ym2 = jnp.where(lane < 2, 0.0, pltpu.roll(c, 2, 1))
            yp1 = jnp.where(lane >= width - 1, 0.0, pltpu.roll(c, width - 1, 1))
            yp2 = jnp.where(lane >= width - 2, 0.0, pltpu.roll(c, width - 2, 1))
            lap = (-sm2 + 16.0 * sm1 - 30.0 * c + 16.0 * sp1 - sp2) / 12.0
            lap = lap + (-zm2 + 16.0 * zm1 - 30.0 * c + 16.0 * zp1 - zp2) / 12.0
            lap = lap + (-ym2 + 16.0 * ym1 - 30.0 * c + 16.0 * yp1 - yp2) / 12.0
            centers.append(c)
            laps.append(lap)
        start = j * rows if isinstance(j, int) else pl.multiple_of(j * rows, rows)
        d = diff_ref[pl.ds(start, rows), :]
        reaction = rate_ref[pl.ds(start, rows), :] * softplus(centers[0]) * softplus(centers[1])
        for s in range(2):
            value = centers[s] + d * laps[s] + reaction_yields[s] * reaction
            for h in range(width // 128):
                ex_ref[s, h, pl.ds(start, rows), :] = value[:, h * 128:(h + 1) * 128]

    for j in (0, 1):
        one_plane(j, j - 2, j - 1, j + 1, j + 2)

    def body(j, carry):
        one_plane(j, j - 2, j - 1, j + 1, j + 2)
        return carry

    lax.fori_loop(2, planes - 2, body, 0)
    for j in (planes - 2, planes - 1):
        one_plane(j, j - 2, j - 1, j + 1, j + 2)

    for s in range(2):
        inv = inv_ref[s]
        for h in range(width // 128):

            def mm(z, carry):
                b = ex_ref[s, h, pl.ds(z, planes, stride=rows), :]
                r = jnp.dot(
                    inv, b, precision=lax.Precision.HIGHEST, preferred_element_type=jnp.float32
                )
                ex_ref[s, h, pl.ds(z, planes, stride=rows), :] = r
                return carry

            lax.fori_loop(0, rows, mm, 0)
            exit_ref[s, :, pl.ds(h * 128, 128)] = ex_ref[s, h, pl.ds((planes - 1) * rows, rows), :]

    chunk = 8 * rows

    def put(c, carry):
        start = pl.multiple_of(c * chunk, chunk)
        for s in range(2):
            for h in range(width // 128):
                out_ref[s, pl.ds(start, chunk), pl.ds(h * 128, 128)] = ex_ref[s, h, pl.ds(start, chunk), :]
        return carry

    lax.fori_loop(0, planes // 8, put, 0)


def explicit_local(scalars, head, tail, before, after, diffusivity, reaction_rate, inverse):
    species, planes, rows, width = scalars.shape
    flat = lambda a: a.reshape(a.shape[:-3] + (a.shape[-3] * rows, width))
    vmem = pl.BlockSpec(memory_space=pltpu.VMEM)
    out, exit_plane = pl.pallas_call(
        functools.partial(explicit_kernel, planes, rows, width),
        out_shape=(
            jax.ShapeDtypeStruct((species, planes * rows, width), jnp.float32),
            jax.ShapeDtypeStruct((species, rows, width), jnp.float32),
        ),
        in_specs=[vmem] * 8,
        out_specs=(vmem, vmem),
        scratch_shapes=[pltpu.VMEM((species, width // 128, planes * rows, 128), jnp.float32)],
        compiler_params=pltpu.CompilerParams(vmem_limit_bytes=60 * 1024 * 1024),
        cost_estimate=pl.CostEstimate(
            flops=species * planes * rows * width * (2 * planes + 60),
            transcendentals=2 * planes * rows * width * 2,
            bytes_accessed=4 * (3 * species + 2) * planes * rows * width,
        ),
    )(flat(scalars), flat(head), flat(tail), before, after, flat(diffusivity), flat(reaction_rate), inverse)
    return out.reshape(scalars.shape), exit_plane


def xor_sum(x, axis):
    devices = lax.axis_size(axis)
    step = 1
    while step < devices:
        pairs = [(i, i ^ step) for i in range(devices)]
        x = x + lax.ppermute(x, axis, pairs)
        step *= 2
    return x


def xor_gather(x, axis, dim):
    devices = lax.axis_size(axis)
    place = lax.axis_index(axis)
    step = 1
    while step < devices:
        pairs = [(i, i ^ step) for i in range(devices)]
        other = lax.ppermute(x, axis, pairs)
        low = (place & step) == 0
        x = jnp.where(
            low, jnp.concatenate([x, other], dim), jnp.concatenate([other, x], dim)
        )
        step *= 2
    return x


def compose(earlier, later):
    return (later[0] * earlier[0], later[0] * earlier[1] + later[1])


def exclusive_scan(part, carried, axis):
    devices = lax.axis_size(axis)
    place = lax.axis_index(axis)
    total = part
    before = (jnp.ones_like(part[0]), jnp.zeros_like(part[1]))
    step = 1
    while step < devices:
        pairs = [(i, i ^ step) for i in range(devices)]
        other = lax.ppermute(jnp.stack(total + (carried,)), axis, pairs)
        carried = carried + other[2]
        other = (other[0], other[1])
        later = (place & step) != 0
        new_before = compose(other, before)
        before = jax.tree.map(lambda a, b: jnp.where(later, a, b), new_before, before)
        total = jax.tree.map(
            lambda a, b: jnp.where(later, a, b), compose(other, total), compose(total, other)
        )
        step *= 2
    return before, carried


def halos(x, axis, dim, width, wrap):
    devices, length = (lax.axis_size(axis), x.shape[dim])
    up = [(i, (i + 1) % devices) for i in range(devices if wrap else devices - 1)]
    down = [(j, i) for i, j in up]
    last = lax.slice_in_dim(x, length - width, length, axis=dim)
    first = lax.slice_in_dim(x, 0, width, axis=dim)
    return lax.ppermute(last, axis, up), lax.ppermute(first, axis, down)


def make_inflow(station_plane, mean_profile, recycle_gain, span_shift):
    span_mean = jnp.mean(station_plane, axis=1, keepdims=True)
    rolled = jnp.roll(station_plane, span_shift[0], axis=1)
    return mean_profile[:, None, :] + recycle_gain[:, None, :] * (rolled - span_mean)


def on_device(
    scalars,
    diffusivity,
    reaction_rate,
    block_inverse,
    block_response,
    mean_profile,
    recycle_gain,
    station_index,
    span_shift,
):
    plane_count = scalars.shape[1]
    span_cells = scalars.shape[2]
    stream_devices = lax.axis_size("gx")
    stream_rank = lax.axis_index("gx")
    span_rank = lax.axis_index("gz")
    at_inlet = stream_rank == 0
    owner_row = station_index[0] // plane_count
    local_plane = station_index[0] - owner_row * plane_count
    own_slice = lax.dynamic_index_in_dim(scalars, local_plane, 1, keepdims=False)
    mine = stream_rank == owner_row
    station_plane = xor_gather(own_slice, "gz", 1)
    inflow_full = make_inflow(station_plane, mean_profile, recycle_gain, span_shift)
    own_inflow = lax.dynamic_slice_in_dim(inflow_full, span_rank * span_cells, span_cells, 1)
    candidate = jnp.where(mine, own_inflow, jnp.zeros_like(own_inflow))
    head_planes, tail_planes = halos(scalars, "gx", 1, 2, False)
    edge_shape = (scalars.shape[0], 2, scalars.shape[2], scalars.shape[3])
    outlet_planes = jnp.broadcast_to(scalars[:, -1:], edge_shape)
    head_planes = jnp.where(at_inlet, jnp.zeros(edge_shape, scalars.dtype), head_planes)
    tail_planes = jnp.where(stream_rank == stream_devices - 1, outlet_planes, tail_planes)
    before_rows, after_rows = halos(scalars, "gz", 2, 2, True)
    inverse = block_inverse[:, 0]
    response = block_response[:, 0]
    first_gain = jnp.where(at_inlet, diffusivity[0] * (15.0 / 12.0), 0.0)
    second_gain = jnp.where(at_inlet, diffusivity[1] * (-1.0 / 12.0), 0.0)
    local_part, exit_plane = explicit_local(
        scalars, head_planes, tail_planes, before_rows, after_rows, diffusivity, reaction_rate, inverse
    )
    exit_gain = (
        response[:, -1][:, None, None]
        + inverse[:, -1, 0][:, None, None] * first_gain
        + inverse[:, -1, 1][:, None, None] * second_gain
    )
    (through, upstream_sum), inflow = exclusive_scan((exit_gain, exit_plane), candidate, "gx")
    incoming = through * inflow + upstream_sum
    first_in = first_gain * inflow
    second_in = second_gain * inflow
    return (
        local_part
        + response[:, :, None, None] * incoming[:, None]
        + inverse[:, :, 0][:, :, None, None] * first_in[:, None]
        + inverse[:, :, 1][:, :, None, None] * second_in[:, None]
    )


def solution(mesh):
    return jax.shard_map(
        on_device,
        mesh=mesh,
        in_specs=(
            P(None, "gx", "gz", None),
            P("gx", "gz", None),
            P("gx", "gz", None),
            P(None, "gx", None, None),
            P(None, "gx", None),
            P(),
            P(),
            P(),
            P(),
        ),
        out_specs=P(None, "gx", "gz", None),
        check_vma=False,
    )
```

```python
import functools

import jax
import jax.numpy as jnp
from jax import lax
from jax.experimental import pallas as pl
from jax.experimental.pallas import tpu as pltpu
from jax.sharding import PartitionSpec as P

reaction_yields = (-1.0, 1.0)


def softplus(v):
    return jnp.maximum(v, 0.0) + jnp.log1p(jnp.exp(-jnp.abs(v)))


def explicit_kernel(planes, rows, width,
                    s_ref, head_ref, tail_ref, before_ref, after_ref, diff_ref, rate_ref, inv_ref,
                    out_ref, exit_ref, ex_ref):
    row = lax.broadcasted_iota(jnp.int32, (rows, width), 0)
    lane = lax.broadcasted_iota(jnp.int32, (rows, width), 1)

    def plane(s, k):
        if isinstance(k, int) and k < 0:
            return head_ref[s, pl.ds((k + 2) * rows, rows), :]
        if isinstance(k, int) and k >= planes:
            return tail_ref[s, pl.ds((k - planes) * rows, rows), :]
        start = k * rows if isinstance(k, int) else pl.multiple_of(k * rows, rows)
        return s_ref[s, pl.ds(start, rows), :]

    def halo_row(ref, s, j, r):
        return jnp.broadcast_to(ref[s, j, pl.ds(r, 1), :], (rows, width))

    def one_plane(j, jm2, jm1, jp1, jp2):
        first_row, second_row = row == 0, row == 1
        last_row, next_to_last_row = row == rows - 1, row == rows - 2
        first_lane, second_lane = lane < 1, lane < 2
        last_lane, next_to_last_lane = lane >= width - 1, lane >= width - 2
        centers = []
        laps = []
        for s in range(2):
            c = plane(s, j)
            sm2, sm1, sp1, sp2 = plane(s, jm2), plane(s, jm1), plane(s, jp1), plane(s, jp2)
            b0, b1 = halo_row(before_ref, s, j, 0), halo_row(before_ref, s, j, 1)
            a0, a1 = halo_row(after_ref, s, j, 0), halo_row(after_ref, s, j, 1)
            zm1 = jnp.where(first_row, b1, pltpu.roll(c, 1, 0))
            zm2 = jnp.where(first_row, b0, jnp.where(second_row, b1, pltpu.roll(c, 2, 0)))
            zp1 = jnp.where(last_row, a0, pltpu.roll(c, rows - 1, 0))
            zp2 = jnp.where(last_row, a1, jnp.where(next_to_last_row, a0, pltpu.roll(c, rows - 2, 0)))
            ym1 = jnp.where(first_lane, 0.0, pltpu.roll(c, 1, 1))
            ym2 = jnp.where(second_lane, 0.0, pltpu.roll(c, 2, 1))
            yp1 = jnp.where(last_lane, 0.0, pltpu.roll(c, width - 1, 1))
            yp2 = jnp.where(next_to_last_lane, 0.0, pltpu.roll(c, width - 2, 1))
            near = (sm1 + sp1) + (zm1 + zp1) + (ym1 + yp1)
            far = (sm2 + sp2) + (zm2 + zp2) + (ym2 + yp2)
            lap = (16.0 * near - far - 90.0 * c) * (1.0 / 12.0)
            centers.append(c)
            laps.append(lap)
        start = j * rows if isinstance(j, int) else pl.multiple_of(j * rows, rows)
        d = diff_ref[pl.ds(start, rows), :]
        reaction = rate_ref[pl.ds(start, rows), :] * softplus(centers[0]) * softplus(centers[1])
        for s in range(2):
            value = centers[s] + d * laps[s] + reaction_yields[s] * reaction
            for h in range(width // 128):
                ex_ref[s, h, pl.ds(start, rows), :] = value[:, h * 128:(h + 1) * 128]

    for j in (0, 1):
        one_plane(j, j - 2, j - 1, j + 1, j + 2)

    def body(j, carry):
        one_plane(j, j - 2, j - 1, j + 1, j + 2)
        return carry

    lax.fori_loop(2, planes - 2, body, 0)
    for j in (planes - 2, planes - 1):
        one_plane(j, j - 2, j - 1, j + 1, j + 2)

    for s in range(2):
        inv = inv_ref[s]
        for h in range(width // 128):

            def mm(z, carry):
                b = ex_ref[s, h, pl.ds(z, planes, stride=rows), :]
                r = jnp.dot(
                    inv, b, precision=lax.Precision.HIGHEST, preferred_element_type=jnp.float32
                )
                ex_ref[s, h, pl.ds(z, planes, stride=rows), :] = r
                return carry

            lax.fori_loop(0, rows, mm, 0)
            exit_ref[s, :, pl.ds(h * 128, 128)] = ex_ref[s, h, pl.ds((planes - 1) * rows, rows), :]

    chunk = 8 * rows

    def put(c, carry):
        start = pl.multiple_of(c * chunk, chunk)
        for s in range(2):
            for h in range(width // 128):
                out_ref[s, pl.ds(start, chunk), pl.ds(h * 128, 128)] = ex_ref[s, h, pl.ds(start, chunk), :]
        return carry

    lax.fori_loop(0, planes // 8, put, 0)


def explicit_local(scalars, head, tail, before, after, diffusivity, reaction_rate, inverse):
    species, planes, rows, width = scalars.shape
    flat = lambda a: a.reshape(a.shape[:-3] + (a.shape[-3] * rows, width))
    vmem = pl.BlockSpec(memory_space=pltpu.VMEM)
    out, exit_plane = pl.pallas_call(
        functools.partial(explicit_kernel, planes, rows, width),
        out_shape=(
            jax.ShapeDtypeStruct((species, planes * rows, width), jnp.float32),
            jax.ShapeDtypeStruct((species, rows, width), jnp.float32),
        ),
        in_specs=[vmem] * 8,
        out_specs=(vmem, vmem),
        scratch_shapes=[pltpu.VMEM((species, width // 128, planes * rows, 128), jnp.float32)],
        compiler_params=pltpu.CompilerParams(vmem_limit_bytes=60 * 1024 * 1024),
        cost_estimate=pl.CostEstimate(
            flops=species * planes * rows * width * (2 * planes + 60),
            transcendentals=2 * planes * rows * width * 2,
            bytes_accessed=4 * (3 * species + 2) * planes * rows * width,
        ),
    )(flat(scalars), flat(head), flat(tail), before, after, flat(diffusivity), flat(reaction_rate), inverse)
    return out.reshape(scalars.shape), exit_plane


def xor_sum(x, axis):
    devices = lax.axis_size(axis)
    step = 1
    while step < devices:
        pairs = [(i, i ^ step) for i in range(devices)]
        x = x + lax.ppermute(x, axis, pairs)
        step *= 2
    return x


def xor_gather(x, axis, dim):
    devices = lax.axis_size(axis)
    place = lax.axis_index(axis)
    step = 1
    while step < devices:
        pairs = [(i, i ^ step) for i in range(devices)]
        other = lax.ppermute(x, axis, pairs)
        low = (place & step) == 0
        x = jnp.where(
            low, jnp.concatenate([x, other], dim), jnp.concatenate([other, x], dim)
        )
        step *= 2
    return x


def compose(earlier, later):
    return (later[0] * earlier[0], later[0] * earlier[1] + later[1])


def exclusive_scan(part, carried, axis):
    devices = lax.axis_size(axis)
    place = lax.axis_index(axis)
    total = part
    before = (jnp.ones_like(part[0]), jnp.zeros_like(part[1]))
    step = 1
    while step < devices:
        pairs = [(i, i ^ step) for i in range(devices)]
        other = lax.ppermute(jnp.stack(total + (carried,)), axis, pairs)
        carried = carried + other[2]
        other = (other[0], other[1])
        later = (place & step) != 0
        new_before = compose(other, before)
        before = jax.tree.map(lambda a, b: jnp.where(later, a, b), new_before, before)
        total = jax.tree.map(
            lambda a, b: jnp.where(later, a, b), compose(other, total), compose(total, other)
        )
        step *= 2
    return before, carried


def halos(x, axis, dim, width, wrap):
    devices, length = (lax.axis_size(axis), x.shape[dim])
    up = [(i, (i + 1) % devices) for i in range(devices if wrap else devices - 1)]
    down = [(j, i) for i, j in up]
    last = lax.slice_in_dim(x, length - width, length, axis=dim)
    first = lax.slice_in_dim(x, 0, width, axis=dim)
    return lax.ppermute(last, axis, up), lax.ppermute(first, axis, down)


def make_inflow(station_plane, mean_profile, recycle_gain, span_shift):
    span_mean = jnp.mean(station_plane, axis=1, keepdims=True)
    rolled = jnp.roll(station_plane, span_shift[0], axis=1)
    return mean_profile[:, None, :] + recycle_gain[:, None, :] * (rolled - span_mean)


def on_device(
    scalars,
    diffusivity,
    reaction_rate,
    block_inverse,
    block_response,
    mean_profile,
    recycle_gain,
    station_index,
    span_shift,
):
    plane_count = scalars.shape[1]
    span_cells = scalars.shape[2]
    stream_devices = lax.axis_size("gx")
    stream_rank = lax.axis_index("gx")
    span_rank = lax.axis_index("gz")
    at_inlet = stream_rank == 0
    owner_row = station_index[0] // plane_count
    local_plane = station_index[0] - owner_row * plane_count
    own_slice = lax.dynamic_index_in_dim(scalars, local_plane, 1, keepdims=False)
    mine = stream_rank == owner_row
    station_plane = xor_gather(own_slice, "gz", 1)
    inflow_full = make_inflow(station_plane, mean_profile, recycle_gain, span_shift)
    own_inflow = lax.dynamic_slice_in_dim(inflow_full, span_rank * span_cells, span_cells, 1)
    candidate = jnp.where(mine, own_inflow, jnp.zeros_like(own_inflow))
    head_planes, tail_planes = halos(scalars, "gx", 1, 2, False)
    edge_shape = (scalars.shape[0], 2, scalars.shape[2], scalars.shape[3])
    outlet_planes = jnp.broadcast_to(scalars[:, -1:], edge_shape)
    head_planes = jnp.where(at_inlet, jnp.zeros(edge_shape, scalars.dtype), head_planes)
    tail_planes = jnp.where(stream_rank == stream_devices - 1, outlet_planes, tail_planes)
    before_rows, after_rows = halos(scalars, "gz", 2, 2, True)
    inverse = block_inverse[:, 0]
    response = block_response[:, 0]
    first_gain = jnp.where(at_inlet, diffusivity[0] * (15.0 / 12.0), 0.0)
    second_gain = jnp.where(at_inlet, diffusivity[1] * (-1.0 / 12.0), 0.0)
    local_part, exit_plane = explicit_local(
        scalars, head_planes, tail_planes, before_rows, after_rows, diffusivity, reaction_rate, inverse
    )
    exit_gain = (
        response[:, -1][:, None, None]
        + inverse[:, -1, 0][:, None, None] * first_gain
        + inverse[:, -1, 1][:, None, None] * second_gain
    )
    (through, upstream_sum), inflow = exclusive_scan((exit_gain, exit_plane), candidate, "gx")
    incoming = through * inflow + upstream_sum
    first_in = first_gain * inflow
    second_in = second_gain * inflow
    return (
        local_part
        + response[:, :, None, None] * incoming[:, None]
        + inverse[:, :, 0][:, :, None, None] * first_in[:, None]
        + inverse[:, :, 1][:, :, None, None] * second_in[:, None]
    )


def solution(mesh):
    return jax.shard_map(
        on_device,
        mesh=mesh,
        in_specs=(
            P(None, "gx", "gz", None),
            P("gx", "gz", None),
            P("gx", "gz", None),
            P(None, "gx", None, None),
            P(None, "gx", None),
            P(),
            P(),
            P(),
            P(),
        ),
        out_specs=P(None, "gx", "gz", None),
        check_vma=False,
    )
```

```python
import functools

import jax
import jax.numpy as jnp
from jax import lax
from jax.experimental import pallas as pl
from jax.experimental.pallas import tpu as pltpu
from jax.sharding import PartitionSpec as P

reaction_yields = (-1.0, 1.0)


def softplus(v):
    return jnp.maximum(v, 0.0) + jnp.log1p(jnp.exp(-jnp.abs(v)))


def explicit_kernel(planes, rows, width,
                    s_ref, head_ref, tail_ref, before_ref, after_ref, diff_ref, rate_ref, inv_ref,
                    out_ref, exit_ref, ex_ref):
    row = lax.broadcasted_iota(jnp.int32, (rows, width), 0)
    lane = lax.broadcasted_iota(jnp.int32, (rows, width), 1)

    def plane(s, k):
        if isinstance(k, int) and k < 0:
            return head_ref[s, pl.ds((k + 2) * rows, rows), :]
        if isinstance(k, int) and k >= planes:
            return tail_ref[s, pl.ds((k - planes) * rows, rows), :]
        start = k * rows if isinstance(k, int) else pl.multiple_of(k * rows, rows)
        return s_ref[s, pl.ds(start, rows), :]

    def halo_row(ref, s, j, r):
        return jnp.broadcast_to(ref[s, j, pl.ds(r, 1), :], (rows, width))

    def one_plane(j, jm2, jm1, jp1, jp2):
        first_row, second_row = row == 0, row == 1
        last_row, next_to_last_row = row == rows - 1, row == rows - 2
        first_lane, second_lane = lane < 1, lane < 2
        last_lane, next_to_last_lane = lane >= width - 1, lane >= width - 2
        centers = []
        laps = []
        for s in range(2):
            c = plane(s, j)
            sm2, sm1, sp1, sp2 = plane(s, jm2), plane(s, jm1), plane(s, jp1), plane(s, jp2)
            b0, b1 = halo_row(before_ref, s, j, 0), halo_row(before_ref, s, j, 1)
            a0, a1 = halo_row(after_ref, s, j, 0), halo_row(after_ref, s, j, 1)
            zm1 = jnp.where(first_row, b1, pltpu.roll(c, 1, 0))
            zm2 = jnp.where(first_row, b0, jnp.where(second_row, b1, pltpu.roll(c, 2, 0)))
            zp1 = jnp.where(last_row, a0, pltpu.roll(c, rows - 1, 0))
            zp2 = jnp.where(last_row, a1, jnp.where(next_to_last_row, a0, pltpu.roll(c, rows - 2, 0)))
            ym1 = jnp.where(first_lane, 0.0, pltpu.roll(c, 1, 1))
            ym2 = jnp.where(second_lane, 0.0, pltpu.roll(c, 2, 1))
            yp1 = jnp.where(last_lane, 0.0, pltpu.roll(c, width - 1, 1))
            yp2 = jnp.where(next_to_last_lane, 0.0, pltpu.roll(c, width - 2, 1))
            near = (sm1 + sp1) + (zm1 + zp1) + (ym1 + yp1)
            far = (sm2 + sp2) + (zm2 + zp2) + (ym2 + yp2)
            lap = (16.0 * near - far - 90.0 * c) * (1.0 / 12.0)
            centers.append(c)
            laps.append(lap)
        start = j * rows if isinstance(j, int) else pl.multiple_of(j * rows, rows)
        d = diff_ref[pl.ds(start, rows), :]
        reaction = rate_ref[pl.ds(start, rows), :] * softplus(centers[0]) * softplus(centers[1])
        for s in range(2):
            value = centers[s] + d * laps[s] + reaction_yields[s] * reaction
            for h in range(width // 128):
                ex_ref[s, h, pl.ds(start, rows), :] = value[:, h * 128:(h + 1) * 128]

    for j in (0, 1):
        one_plane(j, j - 2, j - 1, j + 1, j + 2)

    def body(j, carry):
        one_plane(j, j - 2, j - 1, j + 1, j + 2)
        return carry

    lax.fori_loop(2, planes - 2, body, 0, unroll=4)
    for j in (planes - 2, planes - 1):
        one_plane(j, j - 2, j - 1, j + 1, j + 2)

    for s in range(2):
        inv = inv_ref[s]
        for h in range(width // 128):

            def mm(z, carry):
                b = ex_ref[s, h, pl.ds(z, planes, stride=rows), :]
                r = jnp.dot(
                    inv, b, precision=lax.Precision.HIGHEST, preferred_element_type=jnp.float32
                )
                ex_ref[s, h, pl.ds(z, planes, stride=rows), :] = r
                return carry

            lax.fori_loop(0, rows, mm, 0, unroll=True)
            exit_ref[s, :, pl.ds(h * 128, 128)] = ex_ref[s, h, pl.ds((planes - 1) * rows, rows), :]

    chunk = 8 * rows

    def put(c, carry):
        start = pl.multiple_of(c * chunk, chunk)
        for s in range(2):
            for h in range(width // 128):
                out_ref[s, pl.ds(start, chunk), pl.ds(h * 128, 128)] = ex_ref[s, h, pl.ds(start, chunk), :]
        return carry

    lax.fori_loop(0, planes // 8, put, 0)


def explicit_local(scalars, head, tail, before, after, diffusivity, reaction_rate, inverse):
    species, planes, rows, width = scalars.shape
    flat = lambda a: a.reshape(a.shape[:-3] + (a.shape[-3] * rows, width))
    vmem = pl.BlockSpec(memory_space=pltpu.VMEM)
    out, exit_plane = pl.pallas_call(
        functools.partial(explicit_kernel, planes, rows, width),
        out_shape=(
            jax.ShapeDtypeStruct((species, planes * rows, width), jnp.float32),
            jax.ShapeDtypeStruct((species, rows, width), jnp.float32),
        ),
        in_specs=[vmem] * 8,
        out_specs=(vmem, vmem),
        scratch_shapes=[pltpu.VMEM((species, width // 128, planes * rows, 128), jnp.float32)],
        compiler_params=pltpu.CompilerParams(vmem_limit_bytes=60 * 1024 * 1024),
        cost_estimate=pl.CostEstimate(
            flops=species * planes * rows * width * (2 * planes + 60),
            transcendentals=2 * planes * rows * width * 2,
            bytes_accessed=4 * (3 * species + 2) * planes * rows * width,
        ),
    )(flat(scalars), flat(head), flat(tail), before, after, flat(diffusivity), flat(reaction_rate), inverse)
    return out.reshape(scalars.shape), exit_plane


def xor_sum(x, axis):
    devices = lax.axis_size(axis)
    step = 1
    while step < devices:
        pairs = [(i, i ^ step) for i in range(devices)]
        x = x + lax.ppermute(x, axis, pairs)
        step *= 2
    return x


def xor_gather(x, axis, dim):
    devices = lax.axis_size(axis)
    place = lax.axis_index(axis)
    step = 1
    while step < devices:
        pairs = [(i, i ^ step) for i in range(devices)]
        other = lax.ppermute(x, axis, pairs)
        low = (place & step) == 0
        x = jnp.where(
            low, jnp.concatenate([x, other], dim), jnp.concatenate([other, x], dim)
        )
        step *= 2
    return x


def compose(earlier, later):
    return (later[0] * earlier[0], later[0] * earlier[1] + later[1])


def exclusive_scan(part, carried, axis):
    devices = lax.axis_size(axis)
    place = lax.axis_index(axis)
    total = part
    before = (jnp.ones_like(part[0]), jnp.zeros_like(part[1]))
    step = 1
    while step < devices:
        pairs = [(i, i ^ step) for i in range(devices)]
        other = lax.ppermute(jnp.stack(total + (carried,)), axis, pairs)
        carried = carried + other[2]
        other = (other[0], other[1])
        later = (place & step) != 0
        new_before = compose(other, before)
        before = jax.tree.map(lambda a, b: jnp.where(later, a, b), new_before, before)
        total = jax.tree.map(
            lambda a, b: jnp.where(later, a, b), compose(other, total), compose(total, other)
        )
        step *= 2
    return before, carried


def halos(x, axis, dim, width, wrap):
    devices, length = (lax.axis_size(axis), x.shape[dim])
    up = [(i, (i + 1) % devices) for i in range(devices if wrap else devices - 1)]
    down = [(j, i) for i, j in up]
    last = lax.slice_in_dim(x, length - width, length, axis=dim)
    first = lax.slice_in_dim(x, 0, width, axis=dim)
    return lax.ppermute(last, axis, up), lax.ppermute(first, axis, down)


def make_inflow(station_plane, mean_profile, recycle_gain, span_shift):
    span_mean = jnp.mean(station_plane, axis=1, keepdims=True)
    rolled = jnp.roll(station_plane, span_shift[0], axis=1)
    return mean_profile[:, None, :] + recycle_gain[:, None, :] * (rolled - span_mean)


def on_device(
    scalars,
    diffusivity,
    reaction_rate,
    block_inverse,
    block_response,
    mean_profile,
    recycle_gain,
    station_index,
    span_shift,
):
    plane_count = scalars.shape[1]
    span_cells = scalars.shape[2]
    stream_devices = lax.axis_size("gx")
    stream_rank = lax.axis_index("gx")
    span_rank = lax.axis_index("gz")
    at_inlet = stream_rank == 0
    owner_row = station_index[0] // plane_count
    local_plane = station_index[0] - owner_row * plane_count
    own_slice = lax.dynamic_index_in_dim(scalars, local_plane, 1, keepdims=False)
    mine = stream_rank == owner_row
    station_plane = xor_gather(own_slice, "gz", 1)
    inflow_full = make_inflow(station_plane, mean_profile, recycle_gain, span_shift)
    own_inflow = lax.dynamic_slice_in_dim(inflow_full, span_rank * span_cells, span_cells, 1)
    candidate = jnp.where(mine, own_inflow, jnp.zeros_like(own_inflow))
    head_planes, tail_planes = halos(scalars, "gx", 1, 2, False)
    edge_shape = (scalars.shape[0], 2, scalars.shape[2], scalars.shape[3])
    outlet_planes = jnp.broadcast_to(scalars[:, -1:], edge_shape)
    head_planes = jnp.where(at_inlet, jnp.zeros(edge_shape, scalars.dtype), head_planes)
    tail_planes = jnp.where(stream_rank == stream_devices - 1, outlet_planes, tail_planes)
    before_rows, after_rows = halos(scalars, "gz", 2, 2, True)
    inverse = block_inverse[:, 0]
    response = block_response[:, 0]
    first_gain = jnp.where(at_inlet, diffusivity[0] * (15.0 / 12.0), 0.0)
    second_gain = jnp.where(at_inlet, diffusivity[1] * (-1.0 / 12.0), 0.0)
    local_part, exit_plane = explicit_local(
        scalars, head_planes, tail_planes, before_rows, after_rows, diffusivity, reaction_rate, inverse
    )
    exit_gain = (
        response[:, -1][:, None, None]
        + inverse[:, -1, 0][:, None, None] * first_gain
        + inverse[:, -1, 1][:, None, None] * second_gain
    )
    (through, upstream_sum), inflow = exclusive_scan((exit_gain, exit_plane), candidate, "gx")
    incoming = through * inflow + upstream_sum
    first_in = first_gain * inflow
    second_in = second_gain * inflow
    return (
        local_part
        + response[:, :, None, None] * incoming[:, None]
        + inverse[:, :, 0][:, :, None, None] * first_in[:, None]
        + inverse[:, :, 1][:, :, None, None] * second_in[:, None]
    )


def solution(mesh):
    return jax.shard_map(
        on_device,
        mesh=mesh,
        in_specs=(
            P(None, "gx", "gz", None),
            P("gx", "gz", None),
            P("gx", "gz", None),
            P(None, "gx", None, None),
            P(None, "gx", None),
            P(),
            P(),
            P(),
            P(),
        ),
        out_specs=P(None, "gx", "gz", None),
        check_vma=False,
    )
```

```python
import functools

import jax
import jax.numpy as jnp
from jax import lax
from jax.experimental import pallas as pl
from jax.experimental.pallas import tpu as pltpu
from jax.sharding import PartitionSpec as P

reaction_yields = (-1.0, 1.0)


def softplus(v):
    return jnp.maximum(v, 0.0) + jnp.log1p(jnp.exp(-jnp.abs(v)))


def explicit_kernel(planes, rows, width,
                    s_ref, head_ref, tail_ref, before_ref, after_ref, diff_ref, rate_ref, inv_ref,
                    out_ref, exit_ref, ex_ref):
    row = lax.broadcasted_iota(jnp.int32, (rows, width), 0)
    lane = lax.broadcasted_iota(jnp.int32, (rows, width), 1)

    def plane(s, k):
        if isinstance(k, int) and k < 0:
            return head_ref[s, pl.ds((k + 2) * rows, rows), :]
        if isinstance(k, int) and k >= planes:
            return tail_ref[s, pl.ds((k - planes) * rows, rows), :]
        start = k * rows if isinstance(k, int) else pl.multiple_of(k * rows, rows)
        return s_ref[s, pl.ds(start, rows), :]

    def halo_row(ref, s, j, r):
        return jnp.broadcast_to(ref[s, j, pl.ds(r, 1), :], (rows, width))

    def one_plane(j, jm2, jm1, jp1, jp2):
        first_row, second_row = row == 0, row == 1
        last_row, next_to_last_row = row == rows - 1, row == rows - 2
        first_lane, second_lane = lane < 1, lane < 2
        last_lane, next_to_last_lane = lane >= width - 1, lane >= width - 2
        centers = []
        laps = []
        for s in range(2):
            c = plane(s, j)
            sm2, sm1, sp1, sp2 = plane(s, jm2), plane(s, jm1), plane(s, jp1), plane(s, jp2)
            b0, b1 = halo_row(before_ref, s, j, 0), halo_row(before_ref, s, j, 1)
            a0, a1 = halo_row(after_ref, s, j, 0), halo_row(after_ref, s, j, 1)
            zm1 = jnp.where(first_row, b1, pltpu.roll(c, 1, 0))
            zm2 = jnp.where(first_row, b0, jnp.where(second_row, b1, pltpu.roll(c, 2, 0)))
            zp1 = jnp.where(last_row, a0, pltpu.roll(c, rows - 1, 0))
            zp2 = jnp.where(last_row, a1, jnp.where(next_to_last_row, a0, pltpu.roll(c, rows - 2, 0)))
            ym1 = jnp.where(first_lane, 0.0, pltpu.roll(c, 1, 1))
            ym2 = jnp.where(second_lane, 0.0, pltpu.roll(c, 2, 1))
            yp1 = jnp.where(last_lane, 0.0, pltpu.roll(c, width - 1, 1))
            yp2 = jnp.where(next_to_last_lane, 0.0, pltpu.roll(c, width - 2, 1))
            near = (sm1 + sp1) + (zm1 + zp1) + (ym1 + yp1)
            far = (sm2 + sp2) + (zm2 + zp2) + (ym2 + yp2)
            lap = (16.0 * near - far - 90.0 * c) * (1.0 / 12.0)
            centers.append(c)
            laps.append(lap)
        start = j * rows if isinstance(j, int) else pl.multiple_of(j * rows, rows)
        d = diff_ref[pl.ds(start, rows), :]
        reaction = rate_ref[pl.ds(start, rows), :] * softplus(centers[0]) * softplus(centers[1])
        for s in range(2):
            value = centers[s] + d * laps[s] + reaction_yields[s] * reaction
            for h in range(width // 128):
                ex_ref[s, h, pl.ds(start, rows), :] = value[:, h * 128:(h + 1) * 128]

    for j in (0, 1):
        one_plane(j, j - 2, j - 1, j + 1, j + 2)

    def body(j, carry):
        one_plane(j, j - 2, j - 1, j + 1, j + 2)
        return carry

    lax.fori_loop(2, planes - 2, body, 0, unroll=4)
    for j in (planes - 2, planes - 1):
        one_plane(j, j - 2, j - 1, j + 1, j + 2)

    for s in range(2):
        inv = inv_ref[s]
        for h in range(width // 128):

            def mm(z, carry):
                b = ex_ref[s, h, pl.ds(z, planes, stride=rows), :]
                r = jnp.dot(
                    inv, b, precision=lax.Precision.HIGHEST, preferred_element_type=jnp.float32
                )
                ex_ref[s, h, pl.ds(z, planes, stride=rows), :] = r
                return carry

            lax.fori_loop(0, rows, mm, 0, unroll=True)
            exit_ref[s, :, pl.ds(h * 128, 128)] = ex_ref[s, h, pl.ds((planes - 1) * rows, rows), :]

    chunk = 8 * rows

    def put(c, carry):
        start = pl.multiple_of(c * chunk, chunk)
        for s in range(2):
            for h in range(width // 128):
                out_ref[s, pl.ds(start, chunk), pl.ds(h * 128, 128)] = ex_ref[s, h, pl.ds(start, chunk), :]
        return carry

    lax.fori_loop(0, planes // 8, put, 0)


def explicit_local(scalars, head, tail, before, after, diffusivity, reaction_rate, inverse):
    species, planes, rows, width = scalars.shape
    flat = lambda a: a.reshape(a.shape[:-3] + (a.shape[-3] * rows, width))
    vmem = pl.BlockSpec(memory_space=pltpu.VMEM)
    out, exit_plane = pl.pallas_call(
        functools.partial(explicit_kernel, planes, rows, width),
        out_shape=(
            jax.ShapeDtypeStruct((species, planes * rows, width), jnp.float32),
            jax.ShapeDtypeStruct((species, rows, width), jnp.float32),
        ),
        in_specs=[vmem] * 8,
        out_specs=(vmem, vmem),
        scratch_shapes=[pltpu.VMEM((species, width // 128, planes * rows, 128), jnp.float32)],
        compiler_params=pltpu.CompilerParams(vmem_limit_bytes=60 * 1024 * 1024),
        cost_estimate=pl.CostEstimate(
            flops=species * planes * rows * width * (2 * planes + 60),
            transcendentals=2 * planes * rows * width * 2,
            bytes_accessed=4 * (3 * species + 2) * planes * rows * width,
        ),
    )(flat(scalars), flat(head), flat(tail), before, after, flat(diffusivity), flat(reaction_rate), inverse)
    return out.reshape(scalars.shape), exit_plane


def digit_levels(devices, radices):
    levels, stride = [], 1
    for radix in radices:
        levels.append((stride, radix))
        stride *= radix
    if stride != devices:
        levels, stride = [], 1
        while stride < devices:
            levels.append((stride, 2))
            stride *= 2
    return levels


def digit_exchange(x, axis, stride, radix):
    devices = lax.axis_size(axis)
    digit = (lax.axis_index(axis) // stride) % radix
    received = {}
    for shift in range(1, radix):
        pairs = [
            (i, i + (((i // stride) % radix + shift) % radix - (i // stride) % radix) * stride)
            for i in range(devices)
        ]
        received[shift] = lax.ppermute(x, axis, pairs)
    blocks = []
    for k in range(radix):
        value = x
        for m in range(radix):
            if m != k:
                value = jnp.where(digit == m, received[(m - k) % radix], value)
        blocks.append(value)
    return blocks, digit


def digit_gather(x, axis, levels, dim):
    for stride, radix in levels:
        blocks, _ = digit_exchange(x, axis, stride, radix)
        x = jnp.concatenate(blocks, dim)
    return x


def pick(digit, options):
    value = options[0]
    for m in range(1, len(options)):
        value = jax.tree.map(lambda a, b: jnp.where(digit == m, a, b), options[m], value)
    return value


def compose(earlier, later):
    return (later[0] * earlier[0], later[0] * earlier[1] + later[1])


def exclusive_scan(part, carried, axis, levels):
    total = part
    before = (jnp.ones_like(part[0]), jnp.zeros_like(part[1]))
    for stride, radix in levels:
        blocks, digit = digit_exchange(jnp.stack(total + (carried,)), axis, stride, radix)
        carried = blocks[0][2]
        for block in blocks[1:]:
            carried = carried + block[2]
        prefix = (jnp.ones_like(part[0]), jnp.zeros_like(part[1]))
        prefixes = []
        for block in blocks:
            prefixes.append(prefix)
            prefix = compose(prefix, (block[0], block[1]))
        before = compose(pick(digit, prefixes), before)
        total = prefix
    return before, carried


def halos(x, axis, dim, width, wrap):
    devices, length = (lax.axis_size(axis), x.shape[dim])
    up = [(i, (i + 1) % devices) for i in range(devices if wrap else devices - 1)]
    down = [(j, i) for i, j in up]
    last = lax.slice_in_dim(x, length - width, length, axis=dim)
    first = lax.slice_in_dim(x, 0, width, axis=dim)
    return lax.ppermute(last, axis, up), lax.ppermute(first, axis, down)


def make_inflow(station_plane, mean_profile, recycle_gain, span_shift):
    span_mean = jnp.mean(station_plane, axis=1, keepdims=True)
    rolled = jnp.roll(station_plane, span_shift[0], axis=1)
    return mean_profile[:, None, :] + recycle_gain[:, None, :] * (rolled - span_mean)


def on_device(
    scalars,
    diffusivity,
    reaction_rate,
    block_inverse,
    block_response,
    mean_profile,
    recycle_gain,
    station_index,
    span_shift,
):
    plane_count = scalars.shape[1]
    span_cells = scalars.shape[2]
    stream_devices = lax.axis_size("gx")
    stream_rank = lax.axis_index("gx")
    span_rank = lax.axis_index("gz")
    at_inlet = stream_rank == 0
    owner_row = station_index[0] // plane_count
    local_plane = station_index[0] - owner_row * plane_count
    own_slice = lax.dynamic_index_in_dim(scalars, local_plane, 1, keepdims=False)
    mine = stream_rank == owner_row
    station_plane = digit_gather(own_slice, "gz", digit_levels(lax.axis_size("gz"), (4, 2)), 1)
    inflow_full = make_inflow(station_plane, mean_profile, recycle_gain, span_shift)
    own_inflow = lax.dynamic_slice_in_dim(inflow_full, span_rank * span_cells, span_cells, 1)
    candidate = jnp.where(mine, own_inflow, jnp.zeros_like(own_inflow))
    head_planes, tail_planes = halos(scalars, "gx", 1, 2, False)
    edge_shape = (scalars.shape[0], 2, scalars.shape[2], scalars.shape[3])
    outlet_planes = jnp.broadcast_to(scalars[:, -1:], edge_shape)
    head_planes = jnp.where(at_inlet, jnp.zeros(edge_shape, scalars.dtype), head_planes)
    tail_planes = jnp.where(stream_rank == stream_devices - 1, outlet_planes, tail_planes)
    before_rows, after_rows = halos(scalars, "gz", 2, 2, True)
    inverse = block_inverse[:, 0]
    response = block_response[:, 0]
    first_gain = jnp.where(at_inlet, diffusivity[0] * (15.0 / 12.0), 0.0)
    second_gain = jnp.where(at_inlet, diffusivity[1] * (-1.0 / 12.0), 0.0)
    local_part, exit_plane = explicit_local(
        scalars, head_planes, tail_planes, before_rows, after_rows, diffusivity, reaction_rate, inverse
    )
    exit_gain = (
        response[:, -1][:, None, None]
        + inverse[:, -1, 0][:, None, None] * first_gain
        + inverse[:, -1, 1][:, None, None] * second_gain
    )
    (through, upstream_sum), inflow = exclusive_scan(
        (exit_gain, exit_plane), candidate, "gx", digit_levels(stream_devices, (2, 4, 4))
    )
    incoming = through * inflow + upstream_sum
    first_in = first_gain * inflow
    second_in = second_gain * inflow
    return (
        local_part
        + response[:, :, None, None] * incoming[:, None]
        + inverse[:, :, 0][:, :, None, None] * first_in[:, None]
        + inverse[:, :, 1][:, :, None, None] * second_in[:, None]
    )


def solution(mesh):
    return jax.shard_map(
        on_device,
        mesh=mesh,
        in_specs=(
            P(None, "gx", "gz", None),
            P("gx", "gz", None),
            P("gx", "gz", None),
            P(None, "gx", None, None),
            P(None, "gx", None),
            P(),
            P(),
            P(),
            P(),
        ),
        out_specs=P(None, "gx", "gz", None),
        check_vma=False,
    )
```

```python
import functools

import jax
import jax.numpy as jnp
from jax import lax
from jax.experimental import pallas as pl
from jax.experimental.pallas import tpu as pltpu
from jax.sharding import PartitionSpec as P

reaction_yields = (-1.0, 1.0)


def softplus(v):
    return jnp.maximum(v, 0.0) + jnp.log1p(jnp.exp(-jnp.abs(v)))


def explicit_kernel(planes, rows, width,
                    s_ref, head_ref, tail_ref, diff_ref, rate_ref, inv_ref,
                    out_ref, exit_ref, ex_ref):
    row = lax.broadcasted_iota(jnp.int32, (rows, width), 0)
    lane = lax.broadcasted_iota(jnp.int32, (rows, width), 1)

    def plane(s, k):
        if isinstance(k, int) and k < 0:
            return head_ref[s, pl.ds((k + 2) * rows, rows), :]
        if isinstance(k, int) and k >= planes:
            return tail_ref[s, pl.ds((k - planes) * rows, rows), :]
        start = k * rows if isinstance(k, int) else pl.multiple_of(k * rows, rows)
        return s_ref[s, pl.ds(start, rows), :]

    def one_plane(j, jm2, jm1, jp1, jp2):
        first_row, second_row = row == 0, row == 1
        last_row, next_to_last_row = row == rows - 1, row == rows - 2
        first_lane, second_lane = lane < 1, lane < 2
        last_lane, next_to_last_lane = lane >= width - 1, lane >= width - 2
        centers = []
        laps = []
        for s in range(2):
            c = plane(s, j)
            sm2, sm1, sp1, sp2 = plane(s, jm2), plane(s, jm1), plane(s, jp1), plane(s, jp2)
            zm1 = jnp.where(first_row, 0.0, pltpu.roll(c, 1, 0))
            zm2 = jnp.where(first_row | second_row, 0.0, pltpu.roll(c, 2, 0))
            zp1 = jnp.where(last_row, 0.0, pltpu.roll(c, rows - 1, 0))
            zp2 = jnp.where(last_row | next_to_last_row, 0.0, pltpu.roll(c, rows - 2, 0))
            ym1 = jnp.where(first_lane, 0.0, pltpu.roll(c, 1, 1))
            ym2 = jnp.where(second_lane, 0.0, pltpu.roll(c, 2, 1))
            yp1 = jnp.where(last_lane, 0.0, pltpu.roll(c, width - 1, 1))
            yp2 = jnp.where(next_to_last_lane, 0.0, pltpu.roll(c, width - 2, 1))
            near = (sm1 + sp1) + (zm1 + zp1) + (ym1 + yp1)
            far = (sm2 + sp2) + (zm2 + zp2) + (ym2 + yp2)
            lap = (16.0 * near - far - 90.0 * c) * (1.0 / 12.0)
            centers.append(c)
            laps.append(lap)
        start = j * rows if isinstance(j, int) else pl.multiple_of(j * rows, rows)
        d = diff_ref[pl.ds(start, rows), :]
        reaction = rate_ref[pl.ds(start, rows), :] * softplus(centers[0]) * softplus(centers[1])
        for s in range(2):
            value = centers[s] + d * laps[s] + reaction_yields[s] * reaction
            for h in range(width // 128):
                ex_ref[s, h, pl.ds(start, rows), :] = value[:, h * 128:(h + 1) * 128]

    for j in (0, 1):
        one_plane(j, j - 2, j - 1, j + 1, j + 2)

    def body(j, carry):
        one_plane(j, j - 2, j - 1, j + 1, j + 2)
        return carry

    lax.fori_loop(2, planes - 2, body, 0, unroll=4)
    for j in (planes - 2, planes - 1):
        one_plane(j, j - 2, j - 1, j + 1, j + 2)

    for s in range(2):
        inv = inv_ref[s]
        for h in range(width // 128):

            def mm(z, carry):
                b = ex_ref[s, h, pl.ds(z, planes, stride=rows), :]
                r = jnp.dot(
                    inv, b, precision=lax.Precision.HIGHEST, preferred_element_type=jnp.float32
                )
                ex_ref[s, h, pl.ds(z, planes, stride=rows), :] = r
                return carry

            lax.fori_loop(0, rows, mm, 0, unroll=True)
            exit_ref[s, :, pl.ds(h * 128, 128)] = ex_ref[s, h, pl.ds((planes - 1) * rows, rows), :]

    chunk = 8 * rows

    def put(c, carry):
        start = pl.multiple_of(c * chunk, chunk)
        for s in range(2):
            for h in range(width // 128):
                out_ref[s, pl.ds(start, chunk), pl.ds(h * 128, 128)] = ex_ref[s, h, pl.ds(start, chunk), :]
        return carry

    lax.fori_loop(0, planes // 8, put, 0)


def explicit_local(scalars, head, tail, diffusivity, reaction_rate, inverse):
    species, planes, rows, width = scalars.shape
    flat = lambda a: a.reshape(a.shape[:-3] + (a.shape[-3] * rows, width))
    vmem = pl.BlockSpec(memory_space=pltpu.VMEM)
    out, exit_plane = pl.pallas_call(
        functools.partial(explicit_kernel, planes, rows, width),
        out_shape=(
            jax.ShapeDtypeStruct((species, planes * rows, width), jnp.float32),
            jax.ShapeDtypeStruct((species, rows, width), jnp.float32),
        ),
        in_specs=[vmem] * 6,
        out_specs=(vmem, vmem),
        scratch_shapes=[pltpu.VMEM((species, width // 128, planes * rows, 128), jnp.float32)],
        compiler_params=pltpu.CompilerParams(vmem_limit_bytes=60 * 1024 * 1024),
        cost_estimate=pl.CostEstimate(
            flops=species * planes * rows * width * (2 * planes + 60),
            transcendentals=2 * planes * rows * width * 2,
            bytes_accessed=4 * (3 * species + 2) * planes * rows * width,
        ),
    )(flat(scalars), flat(head), flat(tail), flat(diffusivity), flat(reaction_rate), inverse)
    return out.reshape(scalars.shape), exit_plane


def digit_levels(devices, radices):
    levels, stride = [], 1
    for radix in radices:
        levels.append((stride, radix))
        stride *= radix
    if stride != devices:
        levels, stride = [], 1
        while stride < devices:
            levels.append((stride, 2))
            stride *= 2
    return levels


def digit_exchange(x, axis, stride, radix):
    devices = lax.axis_size(axis)
    digit = (lax.axis_index(axis) // stride) % radix
    received = {}
    for shift in range(1, radix):
        pairs = [
            (i, i + (((i // stride) % radix + shift) % radix - (i // stride) % radix) * stride)
            for i in range(devices)
        ]
        received[shift] = lax.ppermute(x, axis, pairs)
    blocks = []
    for k in range(radix):
        value = x
        for m in range(radix):
            if m != k:
                value = jnp.where(digit == m, received[(m - k) % radix], value)
        blocks.append(value)
    return blocks, digit


def digit_gather(x, axis, levels, dim):
    for stride, radix in levels:
        blocks, _ = digit_exchange(x, axis, stride, radix)
        x = jnp.concatenate(blocks, dim)
    return x


def pick(digit, options):
    value = options[0]
    for m in range(1, len(options)):
        value = jax.tree.map(lambda a, b: jnp.where(digit == m, a, b), options[m], value)
    return value


def compose(earlier, later):
    return (later[0] * earlier[0], later[0] * earlier[1] + later[1])


def exclusive_scan(part, carried, axis, levels):
    total = part
    before = (jnp.ones_like(part[0]), jnp.zeros_like(part[1]))
    for stride, radix in levels:
        blocks, digit = digit_exchange(jnp.stack(total + (carried,)), axis, stride, radix)
        carried = blocks[0][2]
        for block in blocks[1:]:
            carried = carried + block[2]
        prefix = (jnp.ones_like(part[0]), jnp.zeros_like(part[1]))
        prefixes = []
        for block in blocks:
            prefixes.append(prefix)
            prefix = compose(prefix, (block[0], block[1]))
        before = compose(pick(digit, prefixes), before)
        total = prefix
    return before, carried


def halos(x, axis, dim, width, wrap):
    devices, length = (lax.axis_size(axis), x.shape[dim])
    up = [(i, (i + 1) % devices) for i in range(devices if wrap else devices - 1)]
    down = [(j, i) for i, j in up]
    last = lax.slice_in_dim(x, length - width, length, axis=dim)
    first = lax.slice_in_dim(x, 0, width, axis=dim)
    return lax.ppermute(last, axis, up), lax.ppermute(first, axis, down)


def make_inflow(station_plane, mean_profile, recycle_gain, span_shift):
    span_mean = jnp.mean(station_plane, axis=1, keepdims=True)
    rolled = jnp.roll(station_plane, span_shift[0], axis=1)
    return mean_profile[:, None, :] + recycle_gain[:, None, :] * (rolled - span_mean)


def on_device(
    scalars,
    diffusivity,
    reaction_rate,
    block_inverse,
    block_response,
    mean_profile,
    recycle_gain,
    station_index,
    span_shift,
):
    plane_count = scalars.shape[1]
    span_cells = scalars.shape[2]
    stream_devices = lax.axis_size("gx")
    stream_rank = lax.axis_index("gx")
    span_rank = lax.axis_index("gz")
    at_inlet = stream_rank == 0
    owner_row = station_index[0] // plane_count
    local_plane = station_index[0] - owner_row * plane_count
    own_slice = lax.dynamic_index_in_dim(scalars, local_plane, 1, keepdims=False)
    mine = stream_rank == owner_row
    station_plane = digit_gather(own_slice, "gz", digit_levels(lax.axis_size("gz"), (4, 2)), 1)
    inflow_full = make_inflow(station_plane, mean_profile, recycle_gain, span_shift)
    own_inflow = lax.dynamic_slice_in_dim(inflow_full, span_rank * span_cells, span_cells, 1)
    candidate = jnp.where(mine, own_inflow, jnp.zeros_like(own_inflow))
    head_planes, tail_planes = halos(scalars, "gx", 1, 2, False)
    edge_shape = (scalars.shape[0], 2, scalars.shape[2], scalars.shape[3])
    outlet_planes = jnp.broadcast_to(scalars[:, -1:], edge_shape)
    head_planes = jnp.where(at_inlet, jnp.zeros(edge_shape, scalars.dtype), head_planes)
    tail_planes = jnp.where(stream_rank == stream_devices - 1, outlet_planes, tail_planes)
    before_rows, after_rows = halos(scalars, "gz", 2, 2, True)
    inverse = block_inverse[:, 0]
    response = block_response[:, 0]
    first_gain = jnp.where(at_inlet, diffusivity[0] * (15.0 / 12.0), 0.0)
    second_gain = jnp.where(at_inlet, diffusivity[1] * (-1.0 / 12.0), 0.0)
    local_part, exit_plane = explicit_local(
        scalars, head_planes, tail_planes, diffusivity, reaction_rate, inverse
    )
    b0, b1 = before_rows[:, :, 0], before_rows[:, :, 1]
    a0, a1 = after_rows[:, :, 0], after_rows[:, :, 1]
    edge_terms = jnp.stack(
        [
            diffusivity[:, 0] * (16.0 * b1 - b0) * (1.0 / 12.0),
            diffusivity[:, 1] * -b1 * (1.0 / 12.0),
            diffusivity[:, span_cells - 2] * -a0 * (1.0 / 12.0),
            diffusivity[:, span_cells - 1] * (16.0 * a0 - a1) * (1.0 / 12.0),
        ],
        axis=1,
    )
    edge_part = jnp.einsum(
        "sij,skjy->siky", inverse, edge_terms, precision=lax.Precision.HIGHEST
    )
    gap = jnp.zeros(edge_part.shape[:2] + (span_cells - 4,) + edge_part.shape[3:], edge_part.dtype)
    edge_part = jnp.concatenate([edge_part[:, :, :2], gap, edge_part[:, :, 2:]], axis=2)
    exit_plane = exit_plane + edge_part[:, -1]
    exit_gain = (
        response[:, -1][:, None, None]
        + inverse[:, -1, 0][:, None, None] * first_gain
        + inverse[:, -1, 1][:, None, None] * second_gain
    )
    (through, upstream_sum), inflow = exclusive_scan(
        (exit_gain, exit_plane), candidate, "gx", digit_levels(stream_devices, (2, 4, 4))
    )
    incoming = through * inflow + upstream_sum
    first_in = first_gain * inflow
    second_in = second_gain * inflow
    return (
        local_part
        + edge_part
        + response[:, :, None, None] * incoming[:, None]
        + inverse[:, :, 0][:, :, None, None] * first_in[:, None]
        + inverse[:, :, 1][:, :, None, None] * second_in[:, None]
    )


def solution(mesh):
    return jax.shard_map(
        on_device,
        mesh=mesh,
        in_specs=(
            P(None, "gx", "gz", None),
            P("gx", "gz", None),
            P("gx", "gz", None),
            P(None, "gx", None, None),
            P(None, "gx", None),
            P(),
            P(),
            P(),
            P(),
        ),
        out_specs=P(None, "gx", "gz", None),
        check_vma=False,
    )
```

```python
import functools

import jax
import jax.numpy as jnp
from jax import lax
from jax.experimental import pallas as pl
from jax.experimental.pallas import tpu as pltpu
from jax.sharding import PartitionSpec as P

reaction_yields = (-1.0, 1.0)


def softplus(v):
    return jnp.maximum(v, 0.0) + jnp.log1p(jnp.exp(-jnp.abs(v)))


def explicit_kernel(planes, rows, width,
                    s_ref, head_ref, tail_ref, diff_ref, rate_ref, inv_ref,
                    out_ref, exit_ref, ex_ref):
    row = lax.broadcasted_iota(jnp.int32, (rows, width), 0)
    lane = lax.broadcasted_iota(jnp.int32, (rows, width), 1)

    def plane(s, k):
        if isinstance(k, int) and k < 0:
            return head_ref[s, pl.ds((k + 2) * rows, rows), :]
        if isinstance(k, int) and k >= planes:
            return tail_ref[s, pl.ds((k - planes) * rows, rows), :]
        start = k * rows if isinstance(k, int) else pl.multiple_of(k * rows, rows)
        return s_ref[s, pl.ds(start, rows), :]

    def one_plane(j, jm2, jm1, jp1, jp2):
        first_row, second_row = row == 0, row == 1
        last_row, next_to_last_row = row == rows - 1, row == rows - 2
        first_lane, second_lane = lane < 1, lane < 2
        last_lane, next_to_last_lane = lane >= width - 1, lane >= width - 2
        centers = []
        laps = []
        for s in range(2):
            c = plane(s, j)
            sm2, sm1, sp1, sp2 = plane(s, jm2), plane(s, jm1), plane(s, jp1), plane(s, jp2)
            zm1 = jnp.where(first_row, 0.0, pltpu.roll(c, 1, 0))
            zm2 = jnp.where(first_row | second_row, 0.0, pltpu.roll(c, 2, 0))
            zp1 = jnp.where(last_row, 0.0, pltpu.roll(c, rows - 1, 0))
            zp2 = jnp.where(last_row | next_to_last_row, 0.0, pltpu.roll(c, rows - 2, 0))
            ym1 = jnp.where(first_lane, 0.0, pltpu.roll(c, 1, 1))
            ym2 = jnp.where(second_lane, 0.0, pltpu.roll(c, 2, 1))
            yp1 = jnp.where(last_lane, 0.0, pltpu.roll(c, width - 1, 1))
            yp2 = jnp.where(next_to_last_lane, 0.0, pltpu.roll(c, width - 2, 1))
            near = (sm1 + sp1) + (zm1 + zp1) + (ym1 + yp1)
            far = (sm2 + sp2) + (zm2 + zp2) + (ym2 + yp2)
            lap = (16.0 * near - far - 90.0 * c) * (1.0 / 12.0)
            centers.append(c)
            laps.append(lap)
        start = j * rows if isinstance(j, int) else pl.multiple_of(j * rows, rows)
        d = diff_ref[pl.ds(start, rows), :]
        reaction = rate_ref[pl.ds(start, rows), :] * softplus(centers[0]) * softplus(centers[1])
        for s in range(2):
            value = centers[s] + d * laps[s] + reaction_yields[s] * reaction
            for h in range(width // 128):
                ex_ref[s, h, pl.ds(start, rows), :] = value[:, h * 128:(h + 1) * 128]

    for j in (0, 1):
        one_plane(j, j - 2, j - 1, j + 1, j + 2)

    def body(j, carry):
        one_plane(j, j - 2, j - 1, j + 1, j + 2)
        return carry

    lax.fori_loop(2, planes - 2, body, 0, unroll=4)
    for j in (planes - 2, planes - 1):
        one_plane(j, j - 2, j - 1, j + 1, j + 2)

    for s in range(2):
        inv = inv_ref[s]
        for h in range(width // 128):

            def mm(z, carry):
                b = ex_ref[s, h, pl.ds(z, planes, stride=rows), :]
                r = jnp.dot(
                    inv, b, precision=lax.Precision.HIGHEST, preferred_element_type=jnp.float32
                )
                ex_ref[s, h, pl.ds(z, planes, stride=rows), :] = r
                return carry

            lax.fori_loop(0, rows, mm, 0, unroll=True)
            exit_ref[s, :, pl.ds(h * 128, 128)] = ex_ref[s, h, pl.ds((planes - 1) * rows, rows), :]

    chunk = 8 * rows

    def put(c, carry):
        start = pl.multiple_of(c * chunk, chunk)
        for s in range(2):
            for h in range(width // 128):
                out_ref[s, pl.ds(start, chunk), pl.ds(h * 128, 128)] = ex_ref[s, h, pl.ds(start, chunk), :]
        return carry

    lax.fori_loop(0, planes // 8, put, 0)


def explicit_local(scalars, head, tail, diffusivity, reaction_rate, inverse):
    species, planes, rows, width = scalars.shape
    flat = lambda a: a.reshape(a.shape[:-3] + (a.shape[-3] * rows, width))
    vmem = pl.BlockSpec(memory_space=pltpu.VMEM)
    out, exit_plane = pl.pallas_call(
        functools.partial(explicit_kernel, planes, rows, width),
        out_shape=(
            jax.ShapeDtypeStruct((species, planes * rows, width), jnp.float32),
            jax.ShapeDtypeStruct((species, rows, width), jnp.float32),
        ),
        in_specs=[vmem] * 6,
        out_specs=(vmem, vmem),
        scratch_shapes=[pltpu.VMEM((species, width // 128, planes * rows, 128), jnp.float32)],
        compiler_params=pltpu.CompilerParams(vmem_limit_bytes=60 * 1024 * 1024),
        cost_estimate=pl.CostEstimate(
            flops=species * planes * rows * width * (2 * planes + 60),
            transcendentals=2 * planes * rows * width * 2,
            bytes_accessed=4 * (3 * species + 2) * planes * rows * width,
        ),
    )(flat(scalars), flat(head), flat(tail), flat(diffusivity), flat(reaction_rate), inverse)
    return out.reshape(scalars.shape), exit_plane


def digit_levels(devices, radices):
    levels, stride = [], 1
    for radix in radices:
        levels.append((stride, radix))
        stride *= radix
    if stride != devices:
        levels, stride = [], 1
        while stride < devices:
            levels.append((stride, 2))
            stride *= 2
    return levels


def digit_exchange(x, axis, stride, radix):
    devices = lax.axis_size(axis)
    digit = (lax.axis_index(axis) // stride) % radix
    received = {}
    for shift in range(1, radix):
        pairs = [
            (i, i + (((i // stride) % radix + shift) % radix - (i // stride) % radix) * stride)
            for i in range(devices)
        ]
        received[shift] = lax.ppermute(x, axis, pairs)
    blocks = []
    for k in range(radix):
        value = x
        for m in range(radix):
            if m != k:
                value = jnp.where(digit == m, received[(m - k) % radix], value)
        blocks.append(value)
    return blocks, digit


def digit_gather(x, axis, levels, dim):
    for stride, radix in levels:
        blocks, _ = digit_exchange(x, axis, stride, radix)
        x = jnp.concatenate(blocks, dim)
    return x


def pick(digit, options):
    value = options[0]
    for m in range(1, len(options)):
        value = jax.tree.map(lambda a, b: jnp.where(digit == m, a, b), options[m], value)
    return value


def compose(earlier, later):
    return (later[0] * earlier[0], later[0] * earlier[1] + later[1])


def exclusive_scan(part, carried, axis, levels):
    total = part
    before = (jnp.ones_like(part[0]), jnp.zeros_like(part[1]))
    for stride, radix in levels:
        blocks, digit = digit_exchange(jnp.stack(total + (carried,)), axis, stride, radix)
        carried = blocks[0][2]
        for block in blocks[1:]:
            carried = carried + block[2]
        prefix = (jnp.ones_like(part[0]), jnp.zeros_like(part[1]))
        prefixes = []
        for block in blocks:
            prefixes.append(prefix)
            prefix = compose(prefix, (block[0], block[1]))
        before = compose(pick(digit, prefixes), before)
        total = prefix
    return before, carried


def halos(x, axis, dim, width, wrap):
    devices, length = (lax.axis_size(axis), x.shape[dim])
    up = [(i, (i + 1) % devices) for i in range(devices if wrap else devices - 1)]
    down = [(j, i) for i, j in up]
    last = lax.slice_in_dim(x, length - width, length, axis=dim)
    first = lax.slice_in_dim(x, 0, width, axis=dim)
    return lax.ppermute(last, axis, up), lax.ppermute(first, axis, down)


def make_inflow(station_plane, mean_profile, recycle_gain, span_shift):
    span_mean = jnp.mean(station_plane, axis=1, keepdims=True)
    rolled = jnp.roll(station_plane, span_shift[0], axis=1)
    return mean_profile[:, None, :] + recycle_gain[:, None, :] * (rolled - span_mean)


def on_device(
    scalars,
    diffusivity,
    reaction_rate,
    block_inverse,
    block_response,
    mean_profile,
    recycle_gain,
    station_index,
    span_shift,
):
    plane_count = scalars.shape[1]
    span_cells = scalars.shape[2]
    stream_devices = lax.axis_size("gx")
    stream_rank = lax.axis_index("gx")
    span_rank = lax.axis_index("gz")
    at_inlet = stream_rank == 0
    owner_row = station_index[0] // plane_count
    local_plane = station_index[0] - owner_row * plane_count
    own_slice = lax.dynamic_index_in_dim(scalars, local_plane, 1, keepdims=False)
    mine = stream_rank == owner_row
    station_plane = digit_gather(own_slice, "gz", digit_levels(lax.axis_size("gz"), (4, 2)), 1)
    inflow_full = make_inflow(station_plane, mean_profile, recycle_gain, span_shift)
    own_inflow = lax.dynamic_slice_in_dim(inflow_full, span_rank * span_cells, span_cells, 1)
    candidate = jnp.where(mine, own_inflow, jnp.zeros_like(own_inflow))
    head_planes, tail_planes = halos(scalars, "gx", 1, 2, False)
    edge_shape = (scalars.shape[0], 2, scalars.shape[2], scalars.shape[3])
    outlet_planes = jnp.broadcast_to(scalars[:, -1:], edge_shape)
    head_planes = jnp.where(at_inlet, jnp.zeros(edge_shape, scalars.dtype), head_planes)
    tail_planes = jnp.where(stream_rank == stream_devices - 1, outlet_planes, tail_planes)
    h0, h1 = head_planes[:, 0], head_planes[:, 1]
    t0, t1 = tail_planes[:, 0], tail_planes[:, 1]
    stream_terms = (
        diffusivity[0] * (16.0 * h1 - h0) * (1.0 / 12.0),
        diffusivity[1] * -h1 * (1.0 / 12.0),
        diffusivity[plane_count - 2] * -t0 * (1.0 / 12.0),
        diffusivity[plane_count - 1] * (16.0 * t0 - t1) * (1.0 / 12.0),
    )
    stream_planes = (0, 1, plane_count - 2, plane_count - 1)
    no_planes = jnp.zeros(edge_shape, scalars.dtype)
    before_rows, after_rows = halos(scalars, "gz", 2, 2, True)
    inverse = block_inverse[:, 0]
    response = block_response[:, 0]
    first_gain = jnp.where(at_inlet, diffusivity[0] * (15.0 / 12.0), 0.0)
    second_gain = jnp.where(at_inlet, diffusivity[1] * (-1.0 / 12.0), 0.0)
    local_part, exit_plane = explicit_local(
        scalars, no_planes, no_planes, diffusivity, reaction_rate, inverse
    )
    for plane, term in zip(stream_planes, stream_terms):
        exit_plane = exit_plane + inverse[:, -1, plane][:, None, None] * term
    b0, b1 = before_rows[:, :, 0], before_rows[:, :, 1]
    a0, a1 = after_rows[:, :, 0], after_rows[:, :, 1]
    edge_terms = jnp.stack(
        [
            diffusivity[:, 0] * (16.0 * b1 - b0) * (1.0 / 12.0),
            diffusivity[:, 1] * -b1 * (1.0 / 12.0),
            diffusivity[:, span_cells - 2] * -a0 * (1.0 / 12.0),
            diffusivity[:, span_cells - 1] * (16.0 * a0 - a1) * (1.0 / 12.0),
        ],
        axis=1,
    )
    edge_part = jnp.einsum(
        "sij,skjy->siky", inverse, edge_terms, precision=lax.Precision.HIGHEST
    )
    gap = jnp.zeros(edge_part.shape[:2] + (span_cells - 4,) + edge_part.shape[3:], edge_part.dtype)
    edge_part = jnp.concatenate([edge_part[:, :, :2], gap, edge_part[:, :, 2:]], axis=2)
    exit_plane = exit_plane + edge_part[:, -1]
    exit_gain = (
        response[:, -1][:, None, None]
        + inverse[:, -1, 0][:, None, None] * first_gain
        + inverse[:, -1, 1][:, None, None] * second_gain
    )
    (through, upstream_sum), inflow = exclusive_scan(
        (exit_gain, exit_plane), candidate, "gx", digit_levels(stream_devices, (2, 4, 4))
    )
    incoming = through * inflow + upstream_sum
    first_in = first_gain * inflow + stream_terms[0]
    second_in = second_gain * inflow + stream_terms[1]
    return (
        local_part
        + edge_part
        + response[:, :, None, None] * incoming[:, None]
        + inverse[:, :, 0][:, :, None, None] * first_in[:, None]
        + inverse[:, :, 1][:, :, None, None] * second_in[:, None]
        + inverse[:, :, plane_count - 2][:, :, None, None] * stream_terms[2][:, None]
        + inverse[:, :, plane_count - 1][:, :, None, None] * stream_terms[3][:, None]
    )


def solution(mesh):
    return jax.shard_map(
        on_device,
        mesh=mesh,
        in_specs=(
            P(None, "gx", "gz", None),
            P("gx", "gz", None),
            P("gx", "gz", None),
            P(None, "gx", None, None),
            P(None, "gx", None),
            P(),
            P(),
            P(),
            P(),
        ),
        out_specs=P(None, "gx", "gz", None),
        check_vma=False,
    )
```

```python
import functools

import jax
import jax.numpy as jnp
from jax import lax
from jax.experimental import pallas as pl
from jax.experimental.pallas import tpu as pltpu
from jax.sharding import PartitionSpec as P

reaction_yields = (-1.0, 1.0)


def softplus(v):
    return jnp.maximum(v, 0.0) + jnp.log1p(jnp.exp(-jnp.abs(v)))


def explicit_kernel(planes, rows, width,
                    s_ref, head_ref, tail_ref, diff_ref, rate_ref, inv_ref,
                    out_ref, exit_ref, ex_ref):
    row = lax.broadcasted_iota(jnp.int32, (rows, width), 0)
    lane = lax.broadcasted_iota(jnp.int32, (rows, width), 1)

    def plane(s, k):
        if isinstance(k, int) and k < 0:
            return head_ref[s, pl.ds((k + 2) * rows, rows), :]
        if isinstance(k, int) and k >= planes:
            return tail_ref[s, pl.ds((k - planes) * rows, rows), :]
        start = k * rows if isinstance(k, int) else pl.multiple_of(k * rows, rows)
        return s_ref[s, pl.ds(start, rows), :]

    def one_plane(j, jm2, jm1, jp1, jp2):
        first_row, second_row = row == 0, row == 1
        last_row, next_to_last_row = row == rows - 1, row == rows - 2
        first_lane, second_lane = lane < 1, lane < 2
        last_lane, next_to_last_lane = lane >= width - 1, lane >= width - 2
        centers = []
        laps = []
        for s in range(2):
            c = plane(s, j)
            sm2, sm1, sp1, sp2 = plane(s, jm2), plane(s, jm1), plane(s, jp1), plane(s, jp2)
            zm1 = jnp.where(first_row, 0.0, pltpu.roll(c, 1, 0))
            zm2 = jnp.where(first_row | second_row, 0.0, pltpu.roll(c, 2, 0))
            zp1 = jnp.where(last_row, 0.0, pltpu.roll(c, rows - 1, 0))
            zp2 = jnp.where(last_row | next_to_last_row, 0.0, pltpu.roll(c, rows - 2, 0))
            ym1 = jnp.where(first_lane, 0.0, pltpu.roll(c, 1, 1))
            ym2 = jnp.where(second_lane, 0.0, pltpu.roll(c, 2, 1))
            yp1 = jnp.where(last_lane, 0.0, pltpu.roll(c, width - 1, 1))
            yp2 = jnp.where(next_to_last_lane, 0.0, pltpu.roll(c, width - 2, 1))
            near = (sm1 + sp1) + (zm1 + zp1) + (ym1 + yp1)
            far = (sm2 + sp2) + (zm2 + zp2) + (ym2 + yp2)
            lap = (16.0 * near - far - 90.0 * c) * (1.0 / 12.0)
            centers.append(c)
            laps.append(lap)
        start = j * rows if isinstance(j, int) else pl.multiple_of(j * rows, rows)
        d = diff_ref[pl.ds(start, rows), :]
        reaction = rate_ref[pl.ds(start, rows), :] * softplus(centers[0]) * softplus(centers[1])
        for s in range(2):
            value = centers[s] + d * laps[s] + reaction_yields[s] * reaction
            for h in range(width // 128):
                ex_ref[s, h, pl.ds(start, rows), :] = value[:, h * 128:(h + 1) * 128]

    for j in (0, 1):
        one_plane(j, j - 2, j - 1, j + 1, j + 2)

    def body(j, carry):
        one_plane(j, j - 2, j - 1, j + 1, j + 2)
        return carry

    lax.fori_loop(2, planes - 2, body, 0, unroll=8)
    for j in (planes - 2, planes - 1):
        one_plane(j, j - 2, j - 1, j + 1, j + 2)

    for s in range(2):
        inv = inv_ref[s]
        for h in range(width // 128):

            def mm(z, carry):
                b = ex_ref[s, h, pl.ds(z, planes, stride=rows), :]
                r = jnp.dot(
                    inv, b, precision=lax.Precision.HIGHEST, preferred_element_type=jnp.float32
                )
                ex_ref[s, h, pl.ds(z, planes, stride=rows), :] = r
                return carry

            lax.fori_loop(0, rows, mm, 0, unroll=True)
            exit_ref[s, :, pl.ds(h * 128, 128)] = ex_ref[s, h, pl.ds((planes - 1) * rows, rows), :]

    chunk = 8 * rows

    def put(c, carry):
        start = pl.multiple_of(c * chunk, chunk)
        for s in range(2):
            for h in range(width // 128):
                out_ref[s, pl.ds(start, chunk), pl.ds(h * 128, 128)] = ex_ref[s, h, pl.ds(start, chunk), :]
        return carry

    lax.fori_loop(0, planes // 8, put, 0)


def explicit_local(scalars, head, tail, diffusivity, reaction_rate, inverse):
    species, planes, rows, width = scalars.shape
    flat = lambda a: a.reshape(a.shape[:-3] + (a.shape[-3] * rows, width))
    vmem = pl.BlockSpec(memory_space=pltpu.VMEM)
    out, exit_plane = pl.pallas_call(
        functools.partial(explicit_kernel, planes, rows, width),
        out_shape=(
            jax.ShapeDtypeStruct((species, planes * rows, width), jnp.float32),
            jax.ShapeDtypeStruct((species, rows, width), jnp.float32),
        ),
        in_specs=[vmem] * 6,
        out_specs=(vmem, vmem),
        scratch_shapes=[pltpu.VMEM((species, width // 128, planes * rows, 128), jnp.float32)],
        compiler_params=pltpu.CompilerParams(vmem_limit_bytes=60 * 1024 * 1024),
        cost_estimate=pl.CostEstimate(
            flops=species * planes * rows * width * (2 * planes + 60),
            transcendentals=2 * planes * rows * width * 2,
            bytes_accessed=4 * (3 * species + 2) * planes * rows * width,
        ),
    )(flat(scalars), flat(head), flat(tail), flat(diffusivity), flat(reaction_rate), inverse)
    return out.reshape(scalars.shape), exit_plane


def digit_levels(devices, radices):
    levels, stride = [], 1
    for radix in radices:
        levels.append((stride, radix))
        stride *= radix
    if stride != devices:
        levels, stride = [], 1
        while stride < devices:
            levels.append((stride, 2))
            stride *= 2
    return levels


def digit_exchange(x, axis, stride, radix):
    devices = lax.axis_size(axis)
    digit = (lax.axis_index(axis) // stride) % radix
    received = {}
    for shift in range(1, radix):
        pairs = [
            (i, i + (((i // stride) % radix + shift) % radix - (i // stride) % radix) * stride)
            for i in range(devices)
        ]
        received[shift] = lax.ppermute(x, axis, pairs)
    blocks = []
    for k in range(radix):
        value = x
        for m in range(radix):
            if m != k:
                value = jnp.where(digit == m, received[(m - k) % radix], value)
        blocks.append(value)
    return blocks, digit


def digit_gather(x, axis, levels, dim):
    for stride, radix in levels:
        blocks, _ = digit_exchange(x, axis, stride, radix)
        x = jnp.concatenate(blocks, dim)
    return x


def pick(digit, options):
    value = options[0]
    for m in range(1, len(options)):
        value = jax.tree.map(lambda a, b: jnp.where(digit == m, a, b), options[m], value)
    return value


def compose(earlier, later):
    return (later[0] * earlier[0], later[0] * earlier[1] + later[1])


def exclusive_scan(part, carried, axis, levels):
    total = part
    before = (jnp.ones_like(part[0]), jnp.zeros_like(part[1]))
    for stride, radix in levels:
        blocks, digit = digit_exchange(jnp.stack(total + (carried,)), axis, stride, radix)
        carried = blocks[0][2]
        for block in blocks[1:]:
            carried = carried + block[2]
        prefix = (jnp.ones_like(part[0]), jnp.zeros_like(part[1]))
        prefixes = []
        for block in blocks:
            prefixes.append(prefix)
            prefix = compose(prefix, (block[0], block[1]))
        before = compose(pick(digit, prefixes), before)
        total = prefix
    return before, carried


def halos(x, axis, dim, width, wrap):
    devices, length = (lax.axis_size(axis), x.shape[dim])
    up = [(i, (i + 1) % devices) for i in range(devices if wrap else devices - 1)]
    down = [(j, i) for i, j in up]
    last = lax.slice_in_dim(x, length - width, length, axis=dim)
    first = lax.slice_in_dim(x, 0, width, axis=dim)
    return lax.ppermute(last, axis, up), lax.ppermute(first, axis, down)


def make_inflow(station_plane, mean_profile, recycle_gain, span_shift):
    span_mean = jnp.mean(station_plane, axis=1, keepdims=True)
    rolled = jnp.roll(station_plane, span_shift[0], axis=1)
    return mean_profile[:, None, :] + recycle_gain[:, None, :] * (rolled - span_mean)


def on_device(
    scalars,
    diffusivity,
    reaction_rate,
    block_inverse,
    block_response,
    mean_profile,
    recycle_gain,
    station_index,
    span_shift,
):
    plane_count = scalars.shape[1]
    span_cells = scalars.shape[2]
    stream_devices = lax.axis_size("gx")
    stream_rank = lax.axis_index("gx")
    span_rank = lax.axis_index("gz")
    at_inlet = stream_rank == 0
    owner_row = station_index[0] // plane_count
    local_plane = station_index[0] - owner_row * plane_count
    own_slice = lax.dynamic_index_in_dim(scalars, local_plane, 1, keepdims=False)
    mine = stream_rank == owner_row
    station_plane = digit_gather(own_slice, "gz", digit_levels(lax.axis_size("gz"), (4, 2)), 1)
    inflow_full = make_inflow(station_plane, mean_profile, recycle_gain, span_shift)
    own_inflow = lax.dynamic_slice_in_dim(inflow_full, span_rank * span_cells, span_cells, 1)
    candidate = jnp.where(mine, own_inflow, jnp.zeros_like(own_inflow))
    head_planes, tail_planes = halos(scalars, "gx", 1, 2, False)
    edge_shape = (scalars.shape[0], 2, scalars.shape[2], scalars.shape[3])
    outlet_planes = jnp.broadcast_to(scalars[:, -1:], edge_shape)
    head_planes = jnp.where(at_inlet, jnp.zeros(edge_shape, scalars.dtype), head_planes)
    tail_planes = jnp.where(stream_rank == stream_devices - 1, outlet_planes, tail_planes)
    before_rows, after_rows = halos(scalars, "gz", 2, 2, True)
    inverse = block_inverse[:, 0]
    response = block_response[:, 0]
    first_gain = jnp.where(at_inlet, diffusivity[0] * (15.0 / 12.0), 0.0)
    second_gain = jnp.where(at_inlet, diffusivity[1] * (-1.0 / 12.0), 0.0)
    local_part, exit_plane = explicit_local(
        scalars, head_planes, tail_planes, diffusivity, reaction_rate, inverse
    )
    b0, b1 = before_rows[:, :, 0], before_rows[:, :, 1]
    a0, a1 = after_rows[:, :, 0], after_rows[:, :, 1]
    edge_terms = jnp.stack(
        [
            diffusivity[:, 0] * (16.0 * b1 - b0) * (1.0 / 12.0),
            diffusivity[:, 1] * -b1 * (1.0 / 12.0),
            diffusivity[:, span_cells - 2] * -a0 * (1.0 / 12.0),
            diffusivity[:, span_cells - 1] * (16.0 * a0 - a1) * (1.0 / 12.0),
        ],
        axis=1,
    )
    exit_edge = jnp.einsum(
        "sj,skjy->sky", inverse[:, -1], edge_terms, precision=lax.Precision.HIGHEST
    )
    gap = jnp.zeros(exit_edge.shape[:1] + (span_cells - 4,) + exit_edge.shape[2:], exit_edge.dtype)
    exit_plane = exit_plane + jnp.concatenate([exit_edge[:, :2], gap, exit_edge[:, 2:]], axis=1)
    edge_part = jnp.einsum(
        "sij,skjy->siky", inverse, edge_terms, precision=lax.Precision.HIGHEST
    )
    gap = jnp.zeros(edge_part.shape[:2] + (span_cells - 4,) + edge_part.shape[3:], edge_part.dtype)
    edge_part = jnp.concatenate([edge_part[:, :, :2], gap, edge_part[:, :, 2:]], axis=2)
    exit_gain = (
        response[:, -1][:, None, None]
        + inverse[:, -1, 0][:, None, None] * first_gain
        + inverse[:, -1, 1][:, None, None] * second_gain
    )
    (through, upstream_sum), inflow = exclusive_scan(
        (exit_gain, exit_plane), candidate, "gx", digit_levels(stream_devices, (2, 4, 4))
    )
    incoming = through * inflow + upstream_sum
    first_in = first_gain * inflow
    second_in = second_gain * inflow
    return (
        local_part
        + edge_part
        + response[:, :, None, None] * incoming[:, None]
        + inverse[:, :, 0][:, :, None, None] * first_in[:, None]
        + inverse[:, :, 1][:, :, None, None] * second_in[:, None]
    )


def solution(mesh):
    return jax.shard_map(
        on_device,
        mesh=mesh,
        in_specs=(
            P(None, "gx", "gz", None),
            P("gx", "gz", None),
            P("gx", "gz", None),
            P(None, "gx", None, None),
            P(None, "gx", None),
            P(),
            P(),
            P(),
            P(),
        ),
        out_specs=P(None, "gx", "gz", None),
        check_vma=False,
    )
```

```python
import functools

import jax
import jax.numpy as jnp
from jax import lax
from jax.experimental import pallas as pl
from jax.experimental.pallas import tpu as pltpu
from jax.sharding import PartitionSpec as P

reaction_yields = (-1.0, 1.0)


def softplus(v):
    return jnp.maximum(v, 0.0) + jnp.log1p(jnp.exp(-jnp.abs(v)))


def explicit_kernel(planes, rows, width,
                    s_ref, head_ref, tail_ref, diff_ref, rate_ref, inv_ref,
                    out_ref, exit_ref, ex_ref):
    row = lax.broadcasted_iota(jnp.int32, (rows, width), 0)
    lane = lax.broadcasted_iota(jnp.int32, (rows, width), 1)

    def plane(s, k):
        if isinstance(k, int) and k < 0:
            return head_ref[s, pl.ds((k + 2) * rows, rows), :]
        if isinstance(k, int) and k >= planes:
            return tail_ref[s, pl.ds((k - planes) * rows, rows), :]
        start = k * rows if isinstance(k, int) else pl.multiple_of(k * rows, rows)
        return s_ref[s, pl.ds(start, rows), :]

    def one_plane(j, jm2, jm1, jp1, jp2):
        first_row, second_row = row == 0, row == 1
        last_row, next_to_last_row = row == rows - 1, row == rows - 2
        first_lane, second_lane = lane < 1, lane < 2
        last_lane, next_to_last_lane = lane >= width - 1, lane >= width - 2
        centers = []
        laps = []
        for s in range(2):
            c = plane(s, j)
            sm2, sm1, sp1, sp2 = plane(s, jm2), plane(s, jm1), plane(s, jp1), plane(s, jp2)
            zm1 = jnp.where(first_row, 0.0, pltpu.roll(c, 1, 0))
            zm2 = jnp.where(first_row | second_row, 0.0, pltpu.roll(c, 2, 0))
            zp1 = jnp.where(last_row, 0.0, pltpu.roll(c, rows - 1, 0))
            zp2 = jnp.where(last_row | next_to_last_row, 0.0, pltpu.roll(c, rows - 2, 0))
            ym1 = jnp.where(first_lane, 0.0, pltpu.roll(c, 1, 1))
            ym2 = jnp.where(second_lane, 0.0, pltpu.roll(c, 2, 1))
            yp1 = jnp.where(last_lane, 0.0, pltpu.roll(c, width - 1, 1))
            yp2 = jnp.where(next_to_last_lane, 0.0, pltpu.roll(c, width - 2, 1))
            near = (sm1 + sp1) + (zm1 + zp1) + (ym1 + yp1)
            far = (sm2 + sp2) + (zm2 + zp2) + (ym2 + yp2)
            lap = (16.0 * near - far - 90.0 * c) * (1.0 / 12.0)
            centers.append(c)
            laps.append(lap)
        start = j * rows if isinstance(j, int) else pl.multiple_of(j * rows, rows)
        d = diff_ref[pl.ds(start, rows), :]
        reaction = rate_ref[pl.ds(start, rows), :] * softplus(centers[0]) * softplus(centers[1])
        for s in range(2):
            value = centers[s] + d * laps[s] + reaction_yields[s] * reaction
            for h in range(width // 128):
                ex_ref[s, h, pl.ds(start, rows), :] = value[:, h * 128:(h + 1) * 128]

    for j in (0, 1):
        one_plane(j, j - 2, j - 1, j + 1, j + 2)

    def body(j, carry):
        one_plane(j, j - 2, j - 1, j + 1, j + 2)
        return carry

    lax.fori_loop(2, planes - 2, body, 0, unroll=8)
    for j in (planes - 2, planes - 1):
        one_plane(j, j - 2, j - 1, j + 1, j + 2)

    for s in range(2):
        inv = inv_ref[s]
        for h in range(width // 128):

            def mm(z, carry):
                b = ex_ref[s, h, pl.ds(z, planes, stride=rows), :]
                r = jnp.dot(
                    inv, b, precision=lax.Precision.HIGHEST, preferred_element_type=jnp.float32
                )
                ex_ref[s, h, pl.ds(z, planes, stride=rows), :] = r
                return carry

            lax.fori_loop(0, rows, mm, 0, unroll=True)
            exit_ref[s, :, pl.ds(h * 128, 128)] = ex_ref[s, h, pl.ds((planes - 1) * rows, rows), :]

    chunk = 8 * rows

    def put(c, carry):
        start = pl.multiple_of(c * chunk, chunk)
        for s in range(2):
            for h in range(width // 128):
                out_ref[s, pl.ds(start, chunk), pl.ds(h * 128, 128)] = ex_ref[s, h, pl.ds(start, chunk), :]
        return carry

    lax.fori_loop(0, planes // 8, put, 0)


def explicit_local(scalars, head, tail, diffusivity, reaction_rate, inverse):
    species, planes, rows, width = scalars.shape
    flat = lambda a: a.reshape(a.shape[:-3] + (a.shape[-3] * rows, width))
    vmem = pl.BlockSpec(memory_space=pltpu.VMEM)
    out, exit_plane = pl.pallas_call(
        functools.partial(explicit_kernel, planes, rows, width),
        out_shape=(
            jax.ShapeDtypeStruct((species, planes * rows, width), jnp.float32),
            jax.ShapeDtypeStruct((species, rows, width), jnp.float32),
        ),
        in_specs=[vmem] * 6,
        out_specs=(vmem, vmem),
        scratch_shapes=[pltpu.VMEM((species, width // 128, planes * rows, 128), jnp.float32)],
        compiler_params=pltpu.CompilerParams(vmem_limit_bytes=60 * 1024 * 1024),
        cost_estimate=pl.CostEstimate(
            flops=species * planes * rows * width * (2 * planes + 60),
            transcendentals=2 * planes * rows * width * 2,
            bytes_accessed=4 * (3 * species + 2) * planes * rows * width,
        ),
    )(flat(scalars), flat(head), flat(tail), flat(diffusivity), flat(reaction_rate), inverse)
    return out.reshape(scalars.shape), exit_plane


def digit_levels(devices, radices):
    levels, stride = [], 1
    for radix in radices:
        levels.append((stride, radix))
        stride *= radix
    if stride != devices:
        levels, stride = [], 1
        while stride < devices:
            levels.append((stride, 2))
            stride *= 2
    return levels


def digit_exchange(x, axis, stride, radix):
    devices = lax.axis_size(axis)
    digit = (lax.axis_index(axis) // stride) % radix
    received = {}
    for shift in range(1, radix):
        pairs = [
            (i, i + (((i // stride) % radix + shift) % radix - (i // stride) % radix) * stride)
            for i in range(devices)
        ]
        received[shift] = lax.ppermute(x, axis, pairs)
    blocks = []
    for k in range(radix):
        value = x
        for m in range(radix):
            if m != k:
                value = jnp.where(digit == m, received[(m - k) % radix], value)
        blocks.append(value)
    return blocks, digit


def digit_gather(x, axis, levels, dim):
    for stride, radix in levels:
        blocks, _ = digit_exchange(x, axis, stride, radix)
        x = jnp.concatenate(blocks, dim)
    return x


def pick(digit, options):
    value = options[0]
    for m in range(1, len(options)):
        value = jax.tree.map(lambda a, b: jnp.where(digit == m, a, b), options[m], value)
    return value


def compose(earlier, later):
    return (later[0] * earlier[0], later[0] * earlier[1] + later[1])


def exclusive_scan(part, carried, axis, levels):
    total = part
    before = (jnp.ones_like(part[0]), jnp.zeros_like(part[1]))
    for stride, radix in levels:
        blocks, digit = digit_exchange(jnp.stack(total + (carried,)), axis, stride, radix)
        carried = blocks[0][2]
        for block in blocks[1:]:
            carried = carried + block[2]
        prefix = (jnp.ones_like(part[0]), jnp.zeros_like(part[1]))
        prefixes = []
        for block in blocks:
            prefixes.append(prefix)
            prefix = compose(prefix, (block[0], block[1]))
        before = compose(pick(digit, prefixes), before)
        total = prefix
    return before, carried


def halos(x, axis, dim, width, wrap):
    devices, length = (lax.axis_size(axis), x.shape[dim])
    up = [(i, (i + 1) % devices) for i in range(devices if wrap else devices - 1)]
    down = [(j, i) for i, j in up]
    last = lax.slice_in_dim(x, length - width, length, axis=dim)
    first = lax.slice_in_dim(x, 0, width, axis=dim)
    return lax.ppermute(last, axis, up), lax.ppermute(first, axis, down)


def make_inflow(station_plane, mean_profile, recycle_gain, span_shift):
    span_mean = jnp.mean(station_plane, axis=1, keepdims=True)
    rolled = jnp.roll(station_plane, span_shift[0], axis=1)
    return mean_profile[:, None, :] + recycle_gain[:, None, :] * (rolled - span_mean)


def on_device(
    scalars,
    diffusivity,
    reaction_rate,
    block_inverse,
    block_response,
    mean_profile,
    recycle_gain,
    station_index,
    span_shift,
):
    plane_count = scalars.shape[1]
    span_cells = scalars.shape[2]
    stream_devices = lax.axis_size("gx")
    stream_rank = lax.axis_index("gx")
    span_rank = lax.axis_index("gz")
    at_inlet = stream_rank == 0
    owner_row = station_index[0] // plane_count
    local_plane = station_index[0] - owner_row * plane_count
    own_slice = lax.dynamic_index_in_dim(scalars, local_plane, 1, keepdims=False)
    mine = stream_rank == owner_row
    station_plane = digit_gather(own_slice, "gz", digit_levels(lax.axis_size("gz"), (4, 2)), 1)
    inflow_full = make_inflow(station_plane, mean_profile, recycle_gain, span_shift)
    own_inflow = lax.dynamic_slice_in_dim(inflow_full, span_rank * span_cells, span_cells, 1)
    candidate = jnp.where(mine, own_inflow, jnp.zeros_like(own_inflow))
    head_planes, tail_planes = halos(scalars, "gx", 1, 2, False)
    edge_shape = (scalars.shape[0], 2, scalars.shape[2], scalars.shape[3])
    outlet_planes = jnp.broadcast_to(scalars[:, -1:], edge_shape)
    head_planes = jnp.where(at_inlet, jnp.zeros(edge_shape, scalars.dtype), head_planes)
    tail_planes = jnp.where(stream_rank == stream_devices - 1, outlet_planes, tail_planes)
    before_rows, after_rows = halos(scalars, "gz", 2, 2, True)
    inverse = block_inverse[:, 0]
    response = block_response[:, 0]
    first_gain = jnp.where(at_inlet, diffusivity[0] * (15.0 / 12.0), 0.0)
    second_gain = jnp.where(at_inlet, diffusivity[1] * (-1.0 / 12.0), 0.0)
    local_part, exit_plane = explicit_local(
        scalars, head_planes, tail_planes, diffusivity, reaction_rate, inverse
    )
    b0, b1 = before_rows[:, :, 0], before_rows[:, :, 1]
    a0, a1 = after_rows[:, :, 0], after_rows[:, :, 1]
    edge_terms = jnp.stack(
        [
            diffusivity[:, 0] * (16.0 * b1 - b0) * (1.0 / 12.0),
            diffusivity[:, 1] * -b1 * (1.0 / 12.0),
            diffusivity[:, span_cells - 2] * -a0 * (1.0 / 12.0),
            diffusivity[:, span_cells - 1] * (16.0 * a0 - a1) * (1.0 / 12.0),
        ],
        axis=1,
    )
    exit_edge = jnp.einsum(
        "sj,skjy->sky", inverse[:, -1], edge_terms, precision=lax.Precision.HIGHEST
    )
    gap = jnp.zeros(exit_edge.shape[:1] + (span_cells - 4,) + exit_edge.shape[2:], exit_edge.dtype)
    exit_plane = exit_plane + jnp.concatenate([exit_edge[:, :2], gap, exit_edge[:, 2:]], axis=1)
    edge_part = jnp.einsum(
        "sij,skjy->siky", inverse, edge_terms, precision=lax.Precision.HIGHEST
    )
    gap = jnp.zeros(edge_part.shape[:2] + (span_cells - 4,) + edge_part.shape[3:], edge_part.dtype)
    edge_part = jnp.concatenate([edge_part[:, :, :2], gap, edge_part[:, :, 2:]], axis=2)
    exit_gain = (
        response[:, -1][:, None, None]
        + inverse[:, -1, 0][:, None, None] * first_gain
        + inverse[:, -1, 1][:, None, None] * second_gain
    )
    (through, upstream_sum), inflow = exclusive_scan(
        (exit_gain, exit_plane), candidate, "gx", digit_levels(stream_devices, (2, 4, 4))
    )
    incoming = through * inflow + upstream_sum
    first_in = first_gain * inflow
    second_in = second_gain * inflow
    (settled,) = lax.optimization_barrier((local_part + edge_part,))
    return (
        settled
        + response[:, :, None, None] * incoming[:, None]
        + inverse[:, :, 0][:, :, None, None] * first_in[:, None]
        + inverse[:, :, 1][:, :, None, None] * second_in[:, None]
    )


def solution(mesh):
    return jax.shard_map(
        on_device,
        mesh=mesh,
        in_specs=(
            P(None, "gx", "gz", None),
            P("gx", "gz", None),
            P("gx", "gz", None),
            P(None, "gx", None, None),
            P(None, "gx", None),
            P(),
            P(),
            P(),
            P(),
        ),
        out_specs=P(None, "gx", "gz", None),
        check_vma=False,
    )
```

```python
import functools

import jax
import jax.numpy as jnp
from jax import lax
from jax.experimental import pallas as pl
from jax.experimental.pallas import tpu as pltpu
from jax.sharding import PartitionSpec as P

reaction_yields = (-1.0, 1.0)


def softplus(v):
    return jnp.maximum(v, 0.0) + jnp.log1p(jnp.exp(-jnp.abs(v)))


def explicit_kernel(planes, rows, width,
                    s_ref, head_ref, tail_ref, diff_ref, rate_ref, inv_ref,
                    out_ref, exit_ref, rows_ref, ex_ref):
    row = lax.broadcasted_iota(jnp.int32, (rows, width), 0)
    lane = lax.broadcasted_iota(jnp.int32, (rows, width), 1)

    def plane(s, k):
        if isinstance(k, int) and k < 0:
            return head_ref[s, pl.ds((k + 2) * rows, rows), :]
        if isinstance(k, int) and k >= planes:
            return tail_ref[s, pl.ds((k - planes) * rows, rows), :]
        start = k * rows if isinstance(k, int) else pl.multiple_of(k * rows, rows)
        return s_ref[s, pl.ds(start, rows), :]

    def one_plane(j, jm2, jm1, jp1, jp2):
        first_row, second_row = row == 0, row == 1
        last_row, next_to_last_row = row == rows - 1, row == rows - 2
        first_lane, second_lane = lane < 1, lane < 2
        last_lane, next_to_last_lane = lane >= width - 1, lane >= width - 2
        centers = []
        laps = []
        for s in range(2):
            c = plane(s, j)
            sm2, sm1, sp1, sp2 = plane(s, jm2), plane(s, jm1), plane(s, jp1), plane(s, jp2)
            zm1 = jnp.where(first_row, 0.0, pltpu.roll(c, 1, 0))
            zm2 = jnp.where(first_row | second_row, 0.0, pltpu.roll(c, 2, 0))
            zp1 = jnp.where(last_row, 0.0, pltpu.roll(c, rows - 1, 0))
            zp2 = jnp.where(last_row | next_to_last_row, 0.0, pltpu.roll(c, rows - 2, 0))
            ym1 = jnp.where(first_lane, 0.0, pltpu.roll(c, 1, 1))
            ym2 = jnp.where(second_lane, 0.0, pltpu.roll(c, 2, 1))
            yp1 = jnp.where(last_lane, 0.0, pltpu.roll(c, width - 1, 1))
            yp2 = jnp.where(next_to_last_lane, 0.0, pltpu.roll(c, width - 2, 1))
            near = (sm1 + sp1) + (zm1 + zp1) + (ym1 + yp1)
            far = (sm2 + sp2) + (zm2 + zp2) + (ym2 + yp2)
            lap = (16.0 * near - far - 90.0 * c) * (1.0 / 12.0)
            centers.append(c)
            laps.append(lap)
        start = j * rows if isinstance(j, int) else pl.multiple_of(j * rows, rows)
        d = diff_ref[pl.ds(start, rows), :]
        low, high = d[:8], d[rows - 8:]
        edge = jnp.where(row[:8] < 2, low, pltpu.roll(high, 4, 0))
        edge_start = j * 8 if isinstance(j, int) else pl.multiple_of(j * 8, 8)
        rows_ref[pl.ds(edge_start, 8), :] = edge
        reaction = rate_ref[pl.ds(start, rows), :] * softplus(centers[0]) * softplus(centers[1])
        for s in range(2):
            value = centers[s] + d * laps[s] + reaction_yields[s] * reaction
            for h in range(width // 128):
                ex_ref[s, h, pl.ds(start, rows), :] = value[:, h * 128:(h + 1) * 128]

    for j in (0, 1):
        one_plane(j, j - 2, j - 1, j + 1, j + 2)

    def body(j, carry):
        one_plane(j, j - 2, j - 1, j + 1, j + 2)
        return carry

    lax.fori_loop(2, planes - 2, body, 0, unroll=8)
    for j in (planes - 2, planes - 1):
        one_plane(j, j - 2, j - 1, j + 1, j + 2)

    for s in range(2):
        inv = inv_ref[s]
        for h in range(width // 128):

            def mm(z, carry):
                b = ex_ref[s, h, pl.ds(z, planes, stride=rows), :]
                r = jnp.dot(
                    inv, b, precision=lax.Precision.HIGHEST, preferred_element_type=jnp.float32
                )
                ex_ref[s, h, pl.ds(z, planes, stride=rows), :] = r
                return carry

            lax.fori_loop(0, rows, mm, 0, unroll=True)
            exit_ref[s, :, pl.ds(h * 128, 128)] = ex_ref[s, h, pl.ds((planes - 1) * rows, rows), :]

    chunk = 8 * rows

    def put(c, carry):
        start = pl.multiple_of(c * chunk, chunk)
        for s in range(2):
            for h in range(width // 128):
                out_ref[s, pl.ds(start, chunk), pl.ds(h * 128, 128)] = ex_ref[s, h, pl.ds(start, chunk), :]
        return carry

    lax.fori_loop(0, planes // 8, put, 0)


def explicit_local(scalars, head, tail, diffusivity, reaction_rate, inverse):
    species, planes, rows, width = scalars.shape
    flat = lambda a: a.reshape(a.shape[:-3] + (a.shape[-3] * rows, width))
    vmem = pl.BlockSpec(memory_space=pltpu.VMEM)
    out, exit_plane, edge_rows = pl.pallas_call(
        functools.partial(explicit_kernel, planes, rows, width),
        out_shape=(
            jax.ShapeDtypeStruct((species, planes * rows, width), jnp.float32),
            jax.ShapeDtypeStruct((species, rows, width), jnp.float32),
            jax.ShapeDtypeStruct((planes * 8, width), jnp.float32),
        ),
        in_specs=[vmem] * 6,
        out_specs=(vmem, vmem, vmem),
        scratch_shapes=[pltpu.VMEM((species, width // 128, planes * rows, 128), jnp.float32)],
        compiler_params=pltpu.CompilerParams(vmem_limit_bytes=60 * 1024 * 1024),
        cost_estimate=pl.CostEstimate(
            flops=species * planes * rows * width * (2 * planes + 60),
            transcendentals=2 * planes * rows * width * 2,
            bytes_accessed=4 * (3 * species + 2) * planes * rows * width,
        ),
    )(flat(scalars), flat(head), flat(tail), flat(diffusivity), flat(reaction_rate), inverse)
    return out.reshape(scalars.shape), exit_plane, edge_rows.reshape(planes, 8, width)


def digit_levels(devices, radices):
    levels, stride = [], 1
    for radix in radices:
        levels.append((stride, radix))
        stride *= radix
    if stride != devices:
        levels, stride = [], 1
        while stride < devices:
            levels.append((stride, 2))
            stride *= 2
    return levels


def digit_exchange(x, axis, stride, radix):
    devices = lax.axis_size(axis)
    digit = (lax.axis_index(axis) // stride) % radix
    received = {}
    for shift in range(1, radix):
        pairs = [
            (i, i + (((i // stride) % radix + shift) % radix - (i // stride) % radix) * stride)
            for i in range(devices)
        ]
        received[shift] = lax.ppermute(x, axis, pairs)
    blocks = []
    for k in range(radix):
        value = x
        for m in range(radix):
            if m != k:
                value = jnp.where(digit == m, received[(m - k) % radix], value)
        blocks.append(value)
    return blocks, digit


def digit_gather(x, axis, levels, dim):
    for stride, radix in levels:
        blocks, _ = digit_exchange(x, axis, stride, radix)
        x = jnp.concatenate(blocks, dim)
    return x


def pick(digit, options):
    value = options[0]
    for m in range(1, len(options)):
        value = jax.tree.map(lambda a, b: jnp.where(digit == m, a, b), options[m], value)
    return value


def compose(earlier, later):
    return (later[0] * earlier[0], later[0] * earlier[1] + later[1])


def exclusive_scan(part, carried, axis, levels):
    total = part
    before = (jnp.ones_like(part[0]), jnp.zeros_like(part[1]))
    for stride, radix in levels:
        blocks, digit = digit_exchange(jnp.stack(total + (carried,)), axis, stride, radix)
        carried = blocks[0][2]
        for block in blocks[1:]:
            carried = carried + block[2]
        prefix = (jnp.ones_like(part[0]), jnp.zeros_like(part[1]))
        prefixes = []
        for block in blocks:
            prefixes.append(prefix)
            prefix = compose(prefix, (block[0], block[1]))
        before = compose(pick(digit, prefixes), before)
        total = prefix
    return before, carried


def halos(x, axis, dim, width, wrap):
    devices, length = (lax.axis_size(axis), x.shape[dim])
    up = [(i, (i + 1) % devices) for i in range(devices if wrap else devices - 1)]
    down = [(j, i) for i, j in up]
    last = lax.slice_in_dim(x, length - width, length, axis=dim)
    first = lax.slice_in_dim(x, 0, width, axis=dim)
    return lax.ppermute(last, axis, up), lax.ppermute(first, axis, down)


def make_inflow(station_plane, mean_profile, recycle_gain, span_shift):
    span_mean = jnp.mean(station_plane, axis=1, keepdims=True)
    rolled = jnp.roll(station_plane, span_shift[0], axis=1)
    return mean_profile[:, None, :] + recycle_gain[:, None, :] * (rolled - span_mean)


def on_device(
    scalars,
    diffusivity,
    reaction_rate,
    block_inverse,
    block_response,
    mean_profile,
    recycle_gain,
    station_index,
    span_shift,
):
    plane_count = scalars.shape[1]
    span_cells = scalars.shape[2]
    stream_devices = lax.axis_size("gx")
    stream_rank = lax.axis_index("gx")
    span_rank = lax.axis_index("gz")
    at_inlet = stream_rank == 0
    owner_row = station_index[0] // plane_count
    local_plane = station_index[0] - owner_row * plane_count
    own_slice = lax.dynamic_index_in_dim(scalars, local_plane, 1, keepdims=False)
    mine = stream_rank == owner_row
    station_plane = digit_gather(own_slice, "gz", digit_levels(lax.axis_size("gz"), (4, 2)), 1)
    inflow_full = make_inflow(station_plane, mean_profile, recycle_gain, span_shift)
    own_inflow = lax.dynamic_slice_in_dim(inflow_full, span_rank * span_cells, span_cells, 1)
    candidate = jnp.where(mine, own_inflow, jnp.zeros_like(own_inflow))
    head_planes, tail_planes = halos(scalars, "gx", 1, 2, False)
    edge_shape = (scalars.shape[0], 2, scalars.shape[2], scalars.shape[3])
    outlet_planes = jnp.broadcast_to(scalars[:, -1:], edge_shape)
    head_planes = jnp.where(at_inlet, jnp.zeros(edge_shape, scalars.dtype), head_planes)
    tail_planes = jnp.where(stream_rank == stream_devices - 1, outlet_planes, tail_planes)
    before_rows, after_rows = halos(scalars, "gz", 2, 2, True)
    inverse = block_inverse[:, 0]
    response = block_response[:, 0]
    first_gain = jnp.where(at_inlet, diffusivity[0] * (15.0 / 12.0), 0.0)
    second_gain = jnp.where(at_inlet, diffusivity[1] * (-1.0 / 12.0), 0.0)
    local_part, exit_plane, edge_diffusivity = explicit_local(
        scalars, head_planes, tail_planes, diffusivity, reaction_rate, inverse
    )
    b0, b1 = before_rows[:, :, 0], before_rows[:, :, 1]
    a0, a1 = after_rows[:, :, 0], after_rows[:, :, 1]
    edge_terms = jnp.stack(
        [
            edge_diffusivity[:, 0] * (16.0 * b1 - b0) * (1.0 / 12.0),
            edge_diffusivity[:, 1] * -b1 * (1.0 / 12.0),
            edge_diffusivity[:, 2] * -a0 * (1.0 / 12.0),
            edge_diffusivity[:, 3] * (16.0 * a0 - a1) * (1.0 / 12.0),
        ],
        axis=1,
    )
    exit_edge = jnp.einsum(
        "sj,skjy->sky", inverse[:, -1], edge_terms, precision=lax.Precision.HIGHEST
    )
    gap = jnp.zeros(exit_edge.shape[:1] + (span_cells - 4,) + exit_edge.shape[2:], exit_edge.dtype)
    exit_plane = exit_plane + jnp.concatenate([exit_edge[:, :2], gap, exit_edge[:, 2:]], axis=1)
    edge_part = jnp.einsum(
        "sij,skjy->siky", inverse, edge_terms, precision=lax.Precision.HIGHEST
    )
    gap = jnp.zeros(edge_part.shape[:2] + (span_cells - 4,) + edge_part.shape[3:], edge_part.dtype)
    edge_part = jnp.concatenate([edge_part[:, :, :2], gap, edge_part[:, :, 2:]], axis=2)
    exit_gain = (
        response[:, -1][:, None, None]
        + inverse[:, -1, 0][:, None, None] * first_gain
        + inverse[:, -1, 1][:, None, None] * second_gain
    )
    (through, upstream_sum), inflow = exclusive_scan(
        (exit_gain, exit_plane), candidate, "gx", digit_levels(stream_devices, (2, 4, 4))
    )
    incoming = through * inflow + upstream_sum
    first_in = first_gain * inflow
    second_in = second_gain * inflow
    (settled,) = lax.optimization_barrier((local_part + edge_part,))
    return (
        settled
        + response[:, :, None, None] * incoming[:, None]
        + inverse[:, :, 0][:, :, None, None] * first_in[:, None]
        + inverse[:, :, 1][:, :, None, None] * second_in[:, None]
    )


def solution(mesh):
    return jax.shard_map(
        on_device,
        mesh=mesh,
        in_specs=(
            P(None, "gx", "gz", None),
            P("gx", "gz", None),
            P("gx", "gz", None),
            P(None, "gx", None, None),
            P(None, "gx", None),
            P(),
            P(),
            P(),
            P(),
        ),
        out_specs=P(None, "gx", "gz", None),
        check_vma=False,
    )
```

```python
import functools

import jax
import jax.numpy as jnp
from jax import lax
from jax.experimental import pallas as pl
from jax.experimental.pallas import tpu as pltpu
from jax.sharding import PartitionSpec as P

reaction_yields = (-1.0, 1.0)


def softplus(v):
    return jnp.maximum(v, 0.0) + jnp.log1p(jnp.exp(-jnp.abs(v)))


def explicit_kernel(planes, rows, width,
                    s_ref, head_ref, tail_ref, diff_ref, rate_ref, inv_ref,
                    out_ref, exit_ref, ex_ref, sems):
    row = lax.broadcasted_iota(jnp.int32, (rows, width), 0)
    lane = lax.broadcasted_iota(jnp.int32, (rows, width), 1)

    def plane(s, k):
        if isinstance(k, int) and k < 0:
            return head_ref[s, pl.ds((k + 2) * rows, rows), :]
        if isinstance(k, int) and k >= planes:
            return tail_ref[s, pl.ds((k - planes) * rows, rows), :]
        start = k * rows if isinstance(k, int) else pl.multiple_of(k * rows, rows)
        return s_ref[s, pl.ds(start, rows), :]

    def one_plane(j, jm2, jm1, jp1, jp2):
        first_row, second_row = row == 0, row == 1
        last_row, next_to_last_row = row == rows - 1, row == rows - 2
        first_lane, second_lane = lane < 1, lane < 2
        last_lane, next_to_last_lane = lane >= width - 1, lane >= width - 2
        centers = []
        laps = []
        for s in range(2):
            c = plane(s, j)
            sm2, sm1, sp1, sp2 = plane(s, jm2), plane(s, jm1), plane(s, jp1), plane(s, jp2)
            zm1 = jnp.where(first_row, 0.0, pltpu.roll(c, 1, 0))
            zm2 = jnp.where(first_row | second_row, 0.0, pltpu.roll(c, 2, 0))
            zp1 = jnp.where(last_row, 0.0, pltpu.roll(c, rows - 1, 0))
            zp2 = jnp.where(last_row | next_to_last_row, 0.0, pltpu.roll(c, rows - 2, 0))
            ym1 = jnp.where(first_lane, 0.0, pltpu.roll(c, 1, 1))
            ym2 = jnp.where(second_lane, 0.0, pltpu.roll(c, 2, 1))
            yp1 = jnp.where(last_lane, 0.0, pltpu.roll(c, width - 1, 1))
            yp2 = jnp.where(next_to_last_lane, 0.0, pltpu.roll(c, width - 2, 1))
            near = (sm1 + sp1) + (zm1 + zp1) + (ym1 + yp1)
            far = (sm2 + sp2) + (zm2 + zp2) + (ym2 + yp2)
            lap = (16.0 * near - far - 90.0 * c) * (1.0 / 12.0)
            centers.append(c)
            laps.append(lap)
        start = j * rows if isinstance(j, int) else pl.multiple_of(j * rows, rows)
        d = diff_ref[pl.ds(start, rows), :]
        reaction = rate_ref[pl.ds(start, rows), :] * softplus(centers[0]) * softplus(centers[1])
        for s in range(2):
            value = centers[s] + d * laps[s] + reaction_yields[s] * reaction
            for h in range(width // 128):
                ex_ref[s, h, pl.ds(start, rows), :] = value[:, h * 128:(h + 1) * 128]

    for j in (0, 1):
        one_plane(j, j - 2, j - 1, j + 1, j + 2)

    def body(j, carry):
        one_plane(j, j - 2, j - 1, j + 1, j + 2)
        return carry

    lax.fori_loop(2, planes - 2, body, 0, unroll=8)
    for j in (planes - 2, planes - 1):
        one_plane(j, j - 2, j - 1, j + 1, j + 2)

    copies = []
    for s in range(2):
        inv = inv_ref[s]
        for h in range(width // 128):

            def mm(z, carry):
                b = ex_ref[s, h, pl.ds(z, planes, stride=rows), :]
                r = jnp.dot(
                    inv, b, precision=lax.Precision.HIGHEST, preferred_element_type=jnp.float32
                )
                ex_ref[s, h, pl.ds(z, planes, stride=rows), :] = r
                return carry

            lax.fori_loop(0, rows, mm, 0, unroll=True)
            exit_ref[s, :, pl.ds(h * 128, 128)] = ex_ref[s, h, pl.ds((planes - 1) * rows, rows), :]
            copy = pltpu.make_async_copy(
                ex_ref.at[s, h], out_ref.at[s, :, pl.ds(h * 128, 128)], sems.at[len(copies)]
            )
            copy.start()
            copies.append(copy)
    for copy in copies:
        copy.wait()


def explicit_local(scalars, head, tail, diffusivity, reaction_rate, inverse):
    species, planes, rows, width = scalars.shape
    flat = lambda a: a.reshape(a.shape[:-3] + (a.shape[-3] * rows, width))
    vmem = pl.BlockSpec(memory_space=pltpu.VMEM)
    out, exit_plane = pl.pallas_call(
        functools.partial(explicit_kernel, planes, rows, width),
        out_shape=(
            jax.ShapeDtypeStruct((species, planes * rows, width), jnp.float32),
            jax.ShapeDtypeStruct((species, rows, width), jnp.float32),
        ),
        in_specs=[vmem] * 6,
        out_specs=(pl.BlockSpec(memory_space=pl.ANY), vmem),
        scratch_shapes=[
            pltpu.VMEM((species, width // 128, planes * rows, 128), jnp.float32),
            pltpu.SemaphoreType.DMA((species * (width // 128),)),
        ],
        compiler_params=pltpu.CompilerParams(vmem_limit_bytes=60 * 1024 * 1024),
        cost_estimate=pl.CostEstimate(
            flops=species * planes * rows * width * (2 * planes + 60),
            transcendentals=2 * planes * rows * width * 2,
            bytes_accessed=4 * (3 * species + 2) * planes * rows * width,
        ),
    )(flat(scalars), flat(head), flat(tail), flat(diffusivity), flat(reaction_rate), inverse)
    return out.reshape(scalars.shape), exit_plane


def digit_levels(devices, radices):
    levels, stride = [], 1
    for radix in radices:
        levels.append((stride, radix))
        stride *= radix
    if stride != devices:
        levels, stride = [], 1
        while stride < devices:
            levels.append((stride, 2))
            stride *= 2
    return levels


def digit_exchange(x, axis, stride, radix):
    devices = lax.axis_size(axis)
    digit = (lax.axis_index(axis) // stride) % radix
    received = {}
    for shift in range(1, radix):
        pairs = [
            (i, i + (((i // stride) % radix + shift) % radix - (i // stride) % radix) * stride)
            for i in range(devices)
        ]
        received[shift] = lax.ppermute(x, axis, pairs)
    blocks = []
    for k in range(radix):
        value = x
        for m in range(radix):
            if m != k:
                value = jnp.where(digit == m, received[(m - k) % radix], value)
        blocks.append(value)
    return blocks, digit


def digit_gather(x, axis, levels, dim):
    for stride, radix in levels:
        blocks, _ = digit_exchange(x, axis, stride, radix)
        x = jnp.concatenate(blocks, dim)
    return x


def pick(digit, options):
    value = options[0]
    for m in range(1, len(options)):
        value = jax.tree.map(lambda a, b: jnp.where(digit == m, a, b), options[m], value)
    return value


def compose(earlier, later):
    return (later[0] * earlier[0], later[0] * earlier[1] + later[1])


def exclusive_scan(part, carried, axis, levels):
    total = part
    before = (jnp.ones_like(part[0]), jnp.zeros_like(part[1]))
    for stride, radix in levels:
        blocks, digit = digit_exchange(jnp.stack(total + (carried,)), axis, stride, radix)
        carried = blocks[0][2]
        for block in blocks[1:]:
            carried = carried + block[2]
        prefix = (jnp.ones_like(part[0]), jnp.zeros_like(part[1]))
        prefixes = []
        for block in blocks:
            prefixes.append(prefix)
            prefix = compose(prefix, (block[0], block[1]))
        before = compose(pick(digit, prefixes), before)
        total = prefix
    return before, carried


def halos(x, axis, dim, width, wrap):
    devices, length = (lax.axis_size(axis), x.shape[dim])
    up = [(i, (i + 1) % devices) for i in range(devices if wrap else devices - 1)]
    down = [(j, i) for i, j in up]
    last = lax.slice_in_dim(x, length - width, length, axis=dim)
    first = lax.slice_in_dim(x, 0, width, axis=dim)
    return lax.ppermute(last, axis, up), lax.ppermute(first, axis, down)


def make_inflow(station_plane, mean_profile, recycle_gain, span_shift):
    span_mean = jnp.mean(station_plane, axis=1, keepdims=True)
    rolled = jnp.roll(station_plane, span_shift[0], axis=1)
    return mean_profile[:, None, :] + recycle_gain[:, None, :] * (rolled - span_mean)


def on_device(
    scalars,
    diffusivity,
    reaction_rate,
    block_inverse,
    block_response,
    mean_profile,
    recycle_gain,
    station_index,
    span_shift,
):
    plane_count = scalars.shape[1]
    span_cells = scalars.shape[2]
    stream_devices = lax.axis_size("gx")
    stream_rank = lax.axis_index("gx")
    span_rank = lax.axis_index("gz")
    at_inlet = stream_rank == 0
    owner_row = station_index[0] // plane_count
    local_plane = station_index[0] - owner_row * plane_count
    own_slice = lax.dynamic_index_in_dim(scalars, local_plane, 1, keepdims=False)
    mine = stream_rank == owner_row
    station_plane = digit_gather(own_slice, "gz", digit_levels(lax.axis_size("gz"), (4, 2)), 1)
    inflow_full = make_inflow(station_plane, mean_profile, recycle_gain, span_shift)
    own_inflow = lax.dynamic_slice_in_dim(inflow_full, span_rank * span_cells, span_cells, 1)
    candidate = jnp.where(mine, own_inflow, jnp.zeros_like(own_inflow))
    head_planes, tail_planes = halos(scalars, "gx", 1, 2, False)
    edge_shape = (scalars.shape[0], 2, scalars.shape[2], scalars.shape[3])
    outlet_planes = jnp.broadcast_to(scalars[:, -1:], edge_shape)
    head_planes = jnp.where(at_inlet, jnp.zeros(edge_shape, scalars.dtype), head_planes)
    tail_planes = jnp.where(stream_rank == stream_devices - 1, outlet_planes, tail_planes)
    before_rows, after_rows = halos(scalars, "gz", 2, 2, True)
    inverse = block_inverse[:, 0]
    response = block_response[:, 0]
    first_gain = jnp.where(at_inlet, diffusivity[0] * (15.0 / 12.0), 0.0)
    second_gain = jnp.where(at_inlet, diffusivity[1] * (-1.0 / 12.0), 0.0)
    local_part, exit_plane = explicit_local(
        scalars, head_planes, tail_planes, diffusivity, reaction_rate, inverse
    )
    b0, b1 = before_rows[:, :, 0], before_rows[:, :, 1]
    a0, a1 = after_rows[:, :, 0], after_rows[:, :, 1]
    edge_terms = jnp.stack(
        [
            diffusivity[:, 0] * (16.0 * b1 - b0) * (1.0 / 12.0),
            diffusivity[:, 1] * -b1 * (1.0 / 12.0),
            diffusivity[:, span_cells - 2] * -a0 * (1.0 / 12.0),
            diffusivity[:, span_cells - 1] * (16.0 * a0 - a1) * (1.0 / 12.0),
        ],
        axis=1,
    )
    exit_edge = jnp.einsum(
        "sj,skjy->sky", inverse[:, -1], edge_terms, precision=lax.Precision.HIGHEST
    )
    gap = jnp.zeros(exit_edge.shape[:1] + (span_cells - 4,) + exit_edge.shape[2:], exit_edge.dtype)
    exit_plane = exit_plane + jnp.concatenate([exit_edge[:, :2], gap, exit_edge[:, 2:]], axis=1)
    edge_part = jnp.einsum(
        "sij,skjy->siky", inverse, edge_terms, precision=lax.Precision.HIGHEST
    )
    gap = jnp.zeros(edge_part.shape[:2] + (span_cells - 4,) + edge_part.shape[3:], edge_part.dtype)
    edge_part = jnp.concatenate([edge_part[:, :, :2], gap, edge_part[:, :, 2:]], axis=2)
    exit_gain = (
        response[:, -1][:, None, None]
        + inverse[:, -1, 0][:, None, None] * first_gain
        + inverse[:, -1, 1][:, None, None] * second_gain
    )
    (through, upstream_sum), inflow = exclusive_scan(
        (exit_gain, exit_plane), candidate, "gx", digit_levels(stream_devices, (2, 4, 4))
    )
    incoming = through * inflow + upstream_sum
    first_in = first_gain * inflow
    second_in = second_gain * inflow
    (settled,) = lax.optimization_barrier((local_part + edge_part,))
    return (
        settled
        + response[:, :, None, None] * incoming[:, None]
        + inverse[:, :, 0][:, :, None, None] * first_in[:, None]
        + inverse[:, :, 1][:, :, None, None] * second_in[:, None]
    )


def solution(mesh):
    return jax.shard_map(
        on_device,
        mesh=mesh,
        in_specs=(
            P(None, "gx", "gz", None),
            P("gx", "gz", None),
            P("gx", "gz", None),
            P(None, "gx", None, None),
            P(None, "gx", None),
            P(),
            P(),
            P(),
            P(),
        ),
        out_specs=P(None, "gx", "gz", None),
        check_vma=False,
    )
```

```python
import functools

import jax
import jax.numpy as jnp
from jax import lax
from jax.experimental import pallas as pl
from jax.experimental.pallas import tpu as pltpu
from jax.sharding import PartitionSpec as P

reaction_yields = (-1.0, 1.0)


def softplus(v):
    return jnp.maximum(v, 0.0) + jnp.log1p(jnp.exp(-jnp.abs(v)))


def explicit_kernel(planes, rows, width,
                    s_ref, head_ref, tail_ref, diff_ref, rate_ref, inv_ref,
                    out_ref, exit_ref, ex_ref, sems):
    row = lax.broadcasted_iota(jnp.int32, (rows, width), 0)
    lane = lax.broadcasted_iota(jnp.int32, (rows, width), 1)

    def plane(s, k):
        if isinstance(k, int) and k < 0:
            return head_ref[s, pl.ds((k + 2) * rows, rows), :]
        if isinstance(k, int) and k >= planes:
            return tail_ref[s, pl.ds((k - planes) * rows, rows), :]
        start = k * rows if isinstance(k, int) else pl.multiple_of(k * rows, rows)
        return s_ref[s, pl.ds(start, rows), :]

    def one_plane(j, jm2, jm1, jp1, jp2):
        first_row, second_row = row == 0, row == 1
        last_row, next_to_last_row = row == rows - 1, row == rows - 2
        first_lane, second_lane = lane < 1, lane < 2
        last_lane, next_to_last_lane = lane >= width - 1, lane >= width - 2
        centers = []
        laps = []
        for s in range(2):
            c = plane(s, j)
            sm2, sm1, sp1, sp2 = plane(s, jm2), plane(s, jm1), plane(s, jp1), plane(s, jp2)
            zm1 = jnp.where(first_row, 0.0, pltpu.roll(c, 1, 0))
            zm2 = jnp.where(first_row | second_row, 0.0, pltpu.roll(c, 2, 0))
            zp1 = jnp.where(last_row, 0.0, pltpu.roll(c, rows - 1, 0))
            zp2 = jnp.where(last_row | next_to_last_row, 0.0, pltpu.roll(c, rows - 2, 0))
            ym1 = jnp.where(first_lane, 0.0, pltpu.roll(c, 1, 1))
            ym2 = jnp.where(second_lane, 0.0, pltpu.roll(c, 2, 1))
            yp1 = jnp.where(last_lane, 0.0, pltpu.roll(c, width - 1, 1))
            yp2 = jnp.where(next_to_last_lane, 0.0, pltpu.roll(c, width - 2, 1))
            near = (sm1 + sp1) + (zm1 + zp1) + (ym1 + yp1)
            far = (sm2 + sp2) + (zm2 + zp2) + (ym2 + yp2)
            lap = (16.0 * near - far - 90.0 * c) * (1.0 / 12.0)
            centers.append(c)
            laps.append(lap)
        start = j * rows if isinstance(j, int) else pl.multiple_of(j * rows, rows)
        d = diff_ref[pl.ds(start, rows), :]
        reaction = rate_ref[pl.ds(start, rows), :] * softplus(centers[0]) * softplus(centers[1])
        for s in range(2):
            value = centers[s] + d * laps[s] + reaction_yields[s] * reaction
            for h in range(width // 128):
                ex_ref[s, h, pl.ds(start, rows), :] = value[:, h * 128:(h + 1) * 128]

    for j in (0, 1):
        one_plane(j, j - 2, j - 1, j + 1, j + 2)

    def body(j, carry):
        one_plane(j, j - 2, j - 1, j + 1, j + 2)
        return carry

    lax.fori_loop(2, planes - 2, body, 0, unroll=8)
    for j in (planes - 2, planes - 1):
        one_plane(j, j - 2, j - 1, j + 1, j + 2)

    copies = []
    for s in range(2):
        inv = inv_ref[s]
        for h in range(width // 128):

            def mm(z, carry):
                b = ex_ref[s, h, pl.ds(z, planes, stride=rows), :]
                r = jnp.dot(
                    inv, b, precision=lax.Precision.HIGH, preferred_element_type=jnp.float32
                )
                ex_ref[s, h, pl.ds(z, planes, stride=rows), :] = r
                return carry

            lax.fori_loop(0, rows, mm, 0, unroll=True)
            exit_ref[s, :, pl.ds(h * 128, 128)] = ex_ref[s, h, pl.ds((planes - 1) * rows, rows), :]
            copy = pltpu.make_async_copy(
                ex_ref.at[s, h], out_ref.at[s, :, pl.ds(h * 128, 128)], sems.at[len(copies)]
            )
            copy.start()
            copies.append(copy)
    for copy in copies:
        copy.wait()


def explicit_local(scalars, head, tail, diffusivity, reaction_rate, inverse):
    species, planes, rows, width = scalars.shape
    flat = lambda a: a.reshape(a.shape[:-3] + (a.shape[-3] * rows, width))
    vmem = pl.BlockSpec(memory_space=pltpu.VMEM)
    out, exit_plane = pl.pallas_call(
        functools.partial(explicit_kernel, planes, rows, width),
        out_shape=(
            jax.ShapeDtypeStruct((species, planes * rows, width), jnp.float32),
            jax.ShapeDtypeStruct((species, rows, width), jnp.float32),
        ),
        in_specs=[vmem] * 6,
        out_specs=(pl.BlockSpec(memory_space=pl.ANY), vmem),
        scratch_shapes=[
            pltpu.VMEM((species, width // 128, planes * rows, 128), jnp.float32),
            pltpu.SemaphoreType.DMA((species * (width // 128),)),
        ],
        compiler_params=pltpu.CompilerParams(vmem_limit_bytes=60 * 1024 * 1024),
        cost_estimate=pl.CostEstimate(
            flops=species * planes * rows * width * (2 * planes + 60),
            transcendentals=2 * planes * rows * width * 2,
            bytes_accessed=4 * (3 * species + 2) * planes * rows * width,
        ),
    )(flat(scalars), flat(head), flat(tail), flat(diffusivity), flat(reaction_rate), inverse)
    return out.reshape(scalars.shape), exit_plane


def digit_levels(devices, radices):
    levels, stride = [], 1
    for radix in radices:
        levels.append((stride, radix))
        stride *= radix
    if stride != devices:
        levels, stride = [], 1
        while stride < devices:
            levels.append((stride, 2))
            stride *= 2
    return levels


def digit_exchange(x, axis, stride, radix):
    devices = lax.axis_size(axis)
    digit = (lax.axis_index(axis) // stride) % radix
    received = {}
    for shift in range(1, radix):
        pairs = [
            (i, i + (((i // stride) % radix + shift) % radix - (i // stride) % radix) * stride)
            for i in range(devices)
        ]
        received[shift] = lax.ppermute(x, axis, pairs)
    blocks = []
    for k in range(radix):
        value = x
        for m in range(radix):
            if m != k:
                value = jnp.where(digit == m, received[(m - k) % radix], value)
        blocks.append(value)
    return blocks, digit


def digit_gather(x, axis, levels, dim):
    for stride, radix in levels:
        blocks, _ = digit_exchange(x, axis, stride, radix)
        x = jnp.concatenate(blocks, dim)
    return x


def pick(digit, options):
    value = options[0]
    for m in range(1, len(options)):
        value = jax.tree.map(lambda a, b: jnp.where(digit == m, a, b), options[m], value)
    return value


def compose(earlier, later):
    return (later[0] * earlier[0], later[0] * earlier[1] + later[1])


def exclusive_scan(part, carried, axis, levels):
    total = part
    before = (jnp.ones_like(part[0]), jnp.zeros_like(part[1]))
    for stride, radix in levels:
        blocks, digit = digit_exchange(jnp.stack(total + (carried,)), axis, stride, radix)
        carried = blocks[0][2]
        for block in blocks[1:]:
            carried = carried + block[2]
        prefix = (jnp.ones_like(part[0]), jnp.zeros_like(part[1]))
        prefixes = []
        for block in blocks:
            prefixes.append(prefix)
            prefix = compose(prefix, (block[0], block[1]))
        before = compose(pick(digit, prefixes), before)
        total = prefix
    return before, carried


def halos(x, axis, dim, width, wrap):
    devices, length = (lax.axis_size(axis), x.shape[dim])
    up = [(i, (i + 1) % devices) for i in range(devices if wrap else devices - 1)]
    down = [(j, i) for i, j in up]
    last = lax.slice_in_dim(x, length - width, length, axis=dim)
    first = lax.slice_in_dim(x, 0, width, axis=dim)
    return lax.ppermute(last, axis, up), lax.ppermute(first, axis, down)


def make_inflow(station_plane, mean_profile, recycle_gain, span_shift):
    span_mean = jnp.mean(station_plane, axis=1, keepdims=True)
    rolled = jnp.roll(station_plane, span_shift[0], axis=1)
    return mean_profile[:, None, :] + recycle_gain[:, None, :] * (rolled - span_mean)


def on_device(
    scalars,
    diffusivity,
    reaction_rate,
    block_inverse,
    block_response,
    mean_profile,
    recycle_gain,
    station_index,
    span_shift,
):
    plane_count = scalars.shape[1]
    span_cells = scalars.shape[2]
    stream_devices = lax.axis_size("gx")
    stream_rank = lax.axis_index("gx")
    span_rank = lax.axis_index("gz")
    at_inlet = stream_rank == 0
    owner_row = station_index[0] // plane_count
    local_plane = station_index[0] - owner_row * plane_count
    own_slice = lax.dynamic_index_in_dim(scalars, local_plane, 1, keepdims=False)
    mine = stream_rank == owner_row
    station_plane = digit_gather(own_slice, "gz", digit_levels(lax.axis_size("gz"), (4, 2)), 1)
    inflow_full = make_inflow(station_plane, mean_profile, recycle_gain, span_shift)
    own_inflow = lax.dynamic_slice_in_dim(inflow_full, span_rank * span_cells, span_cells, 1)
    candidate = jnp.where(mine, own_inflow, jnp.zeros_like(own_inflow))
    head_planes, tail_planes = halos(scalars, "gx", 1, 2, False)
    edge_shape = (scalars.shape[0], 2, scalars.shape[2], scalars.shape[3])
    outlet_planes = jnp.broadcast_to(scalars[:, -1:], edge_shape)
    head_planes = jnp.where(at_inlet, jnp.zeros(edge_shape, scalars.dtype), head_planes)
    tail_planes = jnp.where(stream_rank == stream_devices - 1, outlet_planes, tail_planes)
    before_rows, after_rows = halos(scalars, "gz", 2, 2, True)
    inverse = block_inverse[:, 0]
    response = block_response[:, 0]
    first_gain = jnp.where(at_inlet, diffusivity[0] * (15.0 / 12.0), 0.0)
    second_gain = jnp.where(at_inlet, diffusivity[1] * (-1.0 / 12.0), 0.0)
    local_part, exit_plane = explicit_local(
        scalars, head_planes, tail_planes, diffusivity, reaction_rate, inverse
    )
    b0, b1 = before_rows[:, :, 0], before_rows[:, :, 1]
    a0, a1 = after_rows[:, :, 0], after_rows[:, :, 1]
    edge_terms = jnp.stack(
        [
            diffusivity[:, 0] * (16.0 * b1 - b0) * (1.0 / 12.0),
            diffusivity[:, 1] * -b1 * (1.0 / 12.0),
            diffusivity[:, span_cells - 2] * -a0 * (1.0 / 12.0),
            diffusivity[:, span_cells - 1] * (16.0 * a0 - a1) * (1.0 / 12.0),
        ],
        axis=1,
    )
    exit_edge = jnp.einsum(
        "sj,skjy->sky", inverse[:, -1], edge_terms, precision=lax.Precision.HIGHEST
    )
    gap = jnp.zeros(exit_edge.shape[:1] + (span_cells - 4,) + exit_edge.shape[2:], exit_edge.dtype)
    exit_plane = exit_plane + jnp.concatenate([exit_edge[:, :2], gap, exit_edge[:, 2:]], axis=1)
    edge_part = jnp.einsum(
        "sij,skjy->siky", inverse, edge_terms, precision=lax.Precision.HIGHEST
    )
    gap = jnp.zeros(edge_part.shape[:2] + (span_cells - 4,) + edge_part.shape[3:], edge_part.dtype)
    edge_part = jnp.concatenate([edge_part[:, :, :2], gap, edge_part[:, :, 2:]], axis=2)
    exit_gain = (
        response[:, -1][:, None, None]
        + inverse[:, -1, 0][:, None, None] * first_gain
        + inverse[:, -1, 1][:, None, None] * second_gain
    )
    (through, upstream_sum), inflow = exclusive_scan(
        (exit_gain, exit_plane), candidate, "gx", digit_levels(stream_devices, (2, 4, 4))
    )
    incoming = through * inflow + upstream_sum
    first_in = first_gain * inflow
    second_in = second_gain * inflow
    (settled,) = lax.optimization_barrier((local_part + edge_part,))
    return (
        settled
        + response[:, :, None, None] * incoming[:, None]
        + inverse[:, :, 0][:, :, None, None] * first_in[:, None]
        + inverse[:, :, 1][:, :, None, None] * second_in[:, None]
    )


def solution(mesh):
    return jax.shard_map(
        on_device,
        mesh=mesh,
        in_specs=(
            P(None, "gx", "gz", None),
            P("gx", "gz", None),
            P("gx", "gz", None),
            P(None, "gx", None, None),
            P(None, "gx", None),
            P(),
            P(),
            P(),
            P(),
        ),
        out_specs=P(None, "gx", "gz", None),
        check_vma=False,
    )
```
